128 devices in a mesh: src: 16 (over x_lo, z, core), loop: 8 (over x_hi, y).
Axes of the slice: x: 4 (x_hi: 2, x_lo: 2; x = x_hi * 2 + x_lo), y: 4, z: 4, core: 2. Of those that a mesh axis runs over, the one named last changes fastest.
Arguments:
- sources: bfloat16 [65536, 768], P(('src', 'loop')), may hold values from -48 to 48
- log_a: float32 [65536], P(('src', 'loop')), may hold values from -3 to 0
- targets: bfloat16 [128, 512, 768], P('src'), may hold values from -6 to 6
- g_old: bfloat16 [128, 512], P('src'), may hold values from -2.5 to 2.5
- log_b: float32 [128, 512], P('src'), may hold values from -3 to 0
- tile_ids: int32 [128, 16, 2], P(('src', 'loop')), may hold values from 0 to 127, as said below
- live_count: int32 [128, 16], P(('src', 'loop')), may hold values from 1 to 2, as said below
Outputs:
- f_new: float32 [65536], P(('src', 'loop'))
- g_new: float32 [128, 512], P('src')
The draws below stay inside these ranges and needn't reach their ends.
Inputs may be any that keep to these rules, and one draw needn't show every extreme that they name: `tile_ids`: tile ids of one device for index o of src lie in o * 8 to (o + 1) * 8 - 1 and are distinct within that group of 2 slots; every tile is in use in some device's list. `live_count`: every index of src has a full group of 2 slots in use in some device's list.
All inputs are finite; a program needn't handle non-finite values.
Results may differ from the reference program's by a relative error of at most 0.0003.
Values may be sent and summed in bfloat16 or wider, within the bound.
No kernel may reach another device: no remote copies, remote signals or barrier semaphores. Data moves between devices by JAX's collectives and lax.ppermute only.
A program may use at most 128 MiB of HBM per device.

```python
import math
import jax
import jax.numpy as jnp
from jax import lax

D = 768
ROWS = 512
TILE = 512
TILES_OWN = 8
CAP = 2
SOURCES = 65536
NT = 128
N_SRC = 16
DEVICES = 128


def draw_sources(key, part):
    key_values = jax.random.fold_in(key, 0)
    values = jnp.clip(jax.random.normal(key_values, (SOURCES, D), jnp.float32), -6.0, 6.0)
    return values.astype(jnp.bfloat16)


def draw_tile_ids(key, part):
    key_order, key_offset, key_stride = jax.random.split(jax.random.fold_in(key, 11), 3)
    order = jax.random.permutation(key_order, DEVICES)
    offset = jax.random.randint(key_offset, (N_SRC,), 0, TILES_OWN)
    stride = 2 * jax.random.randint(key_stride, (DEVICES, N_SRC), 0, TILES_OWN // 2) + 1
    base = (order[:, None] + offset[None, :]) % TILES_OWN
    slots = jnp.arange(CAP, dtype=jnp.int32)
    local = (base[:, :, None] + slots[None, None, :] * stride[:, :, None]) % TILES_OWN
    owner = jnp.arange(N_SRC, dtype=jnp.int32)
    return (owner[None, :, None] * TILES_OWN + local).astype(jnp.int32)


def draw_live_count(key, part):
    counts = jax.random.randint(jax.random.fold_in(key, 23), (DEVICES, N_SRC), 1, CAP + 1)
    full = jnp.arange(DEVICES)[:, None] % N_SRC == jnp.arange(N_SRC)[None, :]
    return jnp.where(full, CAP, counts).astype(jnp.int32)


def level_of(own_key, shape, cuts, smallest, largest):
    gain = 1.0
    for dim, blocks in cuts:
        steps = jax.random.uniform(jax.random.fold_in(jax.random.fold_in(own_key, 6), dim), (blocks,), jnp.float32, smallest / len(cuts), largest / len(cuts))
        gain = gain * jnp.repeat(jnp.exp(steps), shape[dim] // blocks).reshape((-1,) + (1,) * (len(shape) - 1 - dim))
    return gain


def scatter_about(rng, extent, width, limit, pieces=(), kind=jnp.bfloat16):
    gain = level_of(rng, extent, pieces, -0.22, 0.18) if pieces else 1.0
    values = jax.random.normal(rng, extent, jnp.float32) * width * gain
    return jnp.minimum(jnp.maximum(values, -limit), limit).astype(kind)


def setup_inputs(seed: int = 0) -> dict:
    keys = jax.random.split(jax.random.key(seed), 8)
    sources = draw_sources(jax.random.fold_in(keys[7], 71), 0)
    log_a = jnp.clip(-3.0 + 3.0 * jax.random.uniform(keys[1], (SOURCES,), jnp.float32) ** level_of(keys[1], (SOURCES,), ((0, 128),), -0.2, 0.2), -3.0, 0.0)
    targets = scatter_about(keys[2], (NT, TILE, D), 1.0, 6.0, ((0, 16),))
    g_old = scatter_about(keys[3], (NT, TILE), 0.3, 2.5, ((0, 16),))
    log_b = jnp.clip(-3.0 + 3.0 * jax.random.uniform(keys[4], (NT, TILE), jnp.float32) ** level_of(keys[4], (NT, TILE), ((0, 16),), -0.2, 0.2), -3.0, 0.0)
    tile_ids = draw_tile_ids(jax.random.fold_in(keys[7], 71), 0)
    live_count = draw_live_count(jax.random.fold_in(keys[7], 71), 0)
    return dict(sources=sources, log_a=log_a, targets=targets, g_old=g_old, log_b=log_b, tile_ids=tile_ids, live_count=live_count)


EPSILON = 0.1
VERY_LOW = -1e+30

def similarity(rows, fetched):
    return jnp.einsum('rd,std->rst', rows.astype(jnp.float32), fetched.astype(jnp.float32)) / math.sqrt(D)

def reference(sources, log_a, targets, g_old, log_b, tile_ids, live_count):
    source_blocks = sources.reshape(DEVICES, ROWS, D)
    mass_blocks = log_a.reshape(DEVICES, ROWS)
    id_blocks = tile_ids.reshape(DEVICES, N_SRC * CAP).astype(jnp.int32)
    slot_index = jnp.arange(CAP, dtype=jnp.int32)
    live_blocks = (slot_index[None, None, :] < live_count[:, :, None]).reshape(DEVICES, N_SRC * CAP)
    potential = g_old.astype(jnp.float32)

    def row_step(item):
        rows, masses, idents, live_slots = item
        kernel = similarity(rows, targets[idents])
        logits = (potential[idents][None] + kernel) / EPSILON
        logits = jnp.where(live_slots[None, :, None], logits, VERY_LOW)
        top = lax.optimization_barrier(jnp.max(logits, axis=(1, 2)))
        total = lax.optimization_barrier(jnp.sum(jnp.exp(logits - top[:, None, None]), axis=(1, 2)))
        return EPSILON * masses - EPSILON * (top + jnp.log(total))
    f_blocks = lax.map(row_step, (source_blocks, mass_blocks, id_blocks, live_blocks))

    def column_step(carry, item):
        col_top, col_total = carry
        rows, row_potential, idents, live_slots = item
        kernel = similarity(rows, targets[idents])
        logits = (row_potential[:, None, None] + kernel) / EPSILON
        top = lax.optimization_barrier(jnp.max(logits, axis=0))
        total = lax.optimization_barrier(jnp.sum(jnp.exp(logits - top[None]), axis=0))
        top = jnp.where(live_slots[:, None], top, VERY_LOW)
        total = jnp.where(live_slots[:, None], total, 0.0)
        old_top = col_top[idents]
        new_top = jnp.maximum(old_top, top)
        new_total = col_total[idents] * jnp.exp(old_top - new_top) + total * jnp.exp(top - new_top)
        return ((col_top.at[idents].set(new_top), col_total.at[idents].set(new_total)), None)
    start = (jnp.full((NT, TILE), VERY_LOW, jnp.float32), jnp.zeros((NT, TILE), jnp.float32))
    (col_top, col_total), unused = lax.scan(column_step, start, (source_blocks, f_blocks, id_blocks, live_blocks))
    g_new = EPSILON * log_b - EPSILON * (col_top + jnp.log(col_total))
    return (f_blocks.reshape(SOURCES), g_new)
```

```python
import math

import jax
import jax.numpy as jnp
from jax import lax
from jax.sharding import PartitionSpec as P

EPSILON = 0.1
VERY_LOW = -1e30


def similarity(rows_bf, fetched):
    kernel = jnp.einsum("rd,ctd->rct", rows_bf, fetched, preferred_element_type=jnp.float32)
    return kernel / math.sqrt(rows_bf.shape[1])


def row_part(rows_bf, fetched, potential, live_slots):
    kernel = similarity(rows_bf, fetched)
    logits = (potential.astype(jnp.float32)[None] + kernel) / EPSILON
    logits = jnp.where(live_slots[None, :, None], logits, VERY_LOW)
    top = jnp.max(logits, axis=(1, 2))
    total = jnp.sum(jnp.exp(logits - top[:, None, None]), axis=(1, 2))
    return (top, total)


def col_part(rows_bf, row_potential, fetched, live_slots):
    kernel = similarity(rows_bf, fetched)
    logits = (row_potential[:, None, None] + kernel) / EPSILON
    top = jnp.max(logits, axis=0)
    total = jnp.sum(jnp.exp(logits - top[None]), axis=0)
    top = jnp.where(live_slots[:, None], top, VERY_LOW)
    total = jnp.where(live_slots[:, None], total, 0.0)
    return (top, total)


def local(sources, log_a, targets, g_old, log_b, tile_ids, live_count):
    tiles_own = targets.shape[0]
    width = targets.shape[1]
    slots_per = tile_ids.shape[2]
    me = lax.axis_index("src")
    rows_all = lax.all_gather(sources, "src")
    log_a_all = lax.all_gather(log_a, "src")
    ids_all = lax.all_gather(tile_ids[0], "src")
    live_all = lax.all_gather(live_count[0], "src")
    my_ids = lax.dynamic_index_in_dim(ids_all, me, 1, False) - me * tiles_own
    my_count = lax.dynamic_index_in_dim(live_all, me, 1, False)
    live_slots = jnp.arange(slots_per, dtype=jnp.int32)[None, :] < my_count[:, None]

    def rows_of(item):
        rows_bf, ids, live = item
        return row_part(rows_bf, targets[ids], g_old[ids], live)

    row_top, row_total = lax.map(rows_of, (rows_all, my_ids, live_slots))
    top = lax.pmax(row_top, "src")
    total = lax.psum(row_total * jnp.exp(row_top - top), "src")
    f_all = EPSILON * log_a_all - EPSILON * (top + jnp.log(total))
    f_new = lax.dynamic_index_in_dim(f_all, me, 0, False)

    def cols_of(item):
        rows_bf, f_rows, ids, live = item
        return col_part(rows_bf, f_rows, targets[ids], live)

    col_top, col_total = lax.map(cols_of, (rows_all, f_all, my_ids, live_slots))
    flat_ids = my_ids.reshape(-1)
    flat_top = col_top.reshape(-1, width)
    flat_total = col_total.reshape(-1, width)
    onehot = flat_ids[:, None] == jnp.arange(tiles_own, dtype=jnp.int32)[None, :]
    tile_top = jnp.max(jnp.where(onehot[:, :, None], flat_top[:, None, :], VERY_LOW), axis=0)
    scaled = flat_total[:, None, :] * jnp.exp(
        jnp.minimum(flat_top[:, None, :] - tile_top[None], 0.0)
    )
    tile_total = jnp.sum(jnp.where(onehot[:, :, None], scaled, 0.0), axis=0)
    all_top = lax.pmax(tile_top, "loop")
    all_total = lax.psum(tile_total * jnp.exp(tile_top - all_top), "loop")
    g_new = EPSILON * log_b - EPSILON * (all_top + jnp.log(all_total))
    return (f_new, g_new)


def solution(mesh):
    return jax.shard_map(
        local,
        mesh=mesh,
        in_specs=(
            P(("src", "loop"), None),
            P(("src", "loop")),
            P("src", None, None),
            P("src", None),
            P("src", None),
            P(("src", "loop"), None, None),
            P(("src", "loop"), None),
        ),
        out_specs=(P(("src", "loop")), P("src", None)),
        check_vma=False,
    )
```

```python
import math

import jax
import jax.numpy as jnp
from jax import lax
from jax.experimental import pallas as pl
from jax.experimental.pallas import tpu as pltpu
from jax.sharding import PartitionSpec as P

EPSILON = 0.1
VERY_LOW = -1e30
NT_DIMS = (((1,), (1,)), ((), ()))


def row_kernel(ids_ref, cnt_ref, g_ref, t_ref, x_ref, top_ref, tot_ref, *, scale):
    s = pl.program_id(0)
    c = pl.program_id(1)

    @pl.when(c == 0)
    def _():
        top_ref[...] = jnp.full(top_ref.shape, VERY_LOW, jnp.float32)
        tot_ref[...] = jnp.zeros(tot_ref.shape, jnp.float32)

    @pl.when(c < cnt_ref[s])
    def _():
        kt = lax.dot_general(t_ref[...], x_ref[...], NT_DIMS, preferred_element_type=jnp.float32)
        logits = g_ref[...] + kt * scale
        old = top_ref[...]
        new = jnp.maximum(old, jnp.max(logits, axis=0, keepdims=True))
        tot_ref[...] = tot_ref[...] * jnp.exp(old - new) + jnp.sum(
            jnp.exp(logits - new), axis=0, keepdims=True
        )
        top_ref[...] = new


def col_kernel(ids_ref, cnt_ref, f_ref, x_ref, t_ref, top_ref, tot_ref, *, scale):
    s = pl.program_id(0)
    c = pl.program_id(1)

    @pl.when((s == 0) & (c == 0))
    def _():
        top_ref[...] = jnp.full(top_ref.shape, VERY_LOW, jnp.float32)
        tot_ref[...] = jnp.zeros(tot_ref.shape, jnp.float32)

    @pl.when(c < cnt_ref[s])
    def _():
        k = lax.dot_general(x_ref[...], t_ref[...], NT_DIMS, preferred_element_type=jnp.float32)
        logits = f_ref[...] + k * scale
        t = ids_ref[s, c]
        old = top_ref[t]
        new = jnp.maximum(old, jnp.max(logits, axis=0, keepdims=True))
        tot_ref[t] = tot_ref[t] * jnp.exp(old - new) + jnp.sum(
            jnp.exp(logits - new), axis=0, keepdims=True
        )
        top_ref[t] = new


def pick_tile(s, c, ids_ref, cnt_ref):
    live = c < cnt_ref[s]
    return (jnp.where(live, ids_ref[s, c], ids_ref[s, 0]), 0, 0)


def pass_call(body, ids, cnt, column, x_all, targets, rows, out_rows, scale, transposed):
    blocks, depth = x_all.shape[0], x_all.shape[2]
    slots = ids.shape[1]
    width = targets.shape[1]
    x_spec = pl.BlockSpec((None, rows, depth), lambda s, c, ids_ref, cnt_ref: (s, 0, 0))
    t_spec = pl.BlockSpec((None, width, depth), pick_tile)
    if transposed:
        col_spec = pl.BlockSpec((None, width, 1), pick_tile)
        in_specs = [col_spec, t_spec, x_spec]
        operands = (column, targets, x_all)
        out_spec = pl.BlockSpec((None, 1, rows), lambda s, c, ids_ref, cnt_ref: (s, 0, 0))
        out_shape = jax.ShapeDtypeStruct((out_rows, 1, rows), jnp.float32)
    else:
        col_spec = pl.BlockSpec((None, rows, 1), lambda s, c, ids_ref, cnt_ref: (s, 0, 0))
        in_specs = [col_spec, x_spec, t_spec]
        operands = (column, x_all, targets)
        out_spec = pl.BlockSpec((out_rows, 1, width), lambda s, c, ids_ref, cnt_ref: (0, 0, 0))
        out_shape = jax.ShapeDtypeStruct((out_rows, 1, width), jnp.float32)
    flops = 2 * blocks * slots * rows * width * depth
    cost = pl.CostEstimate(
        flops=flops,
        transcendentals=blocks * slots * rows * width,
        bytes_accessed=2 * (x_all.size + blocks * slots * width * depth),
    )
    return pl.pallas_call(
        lambda *refs: body(*refs, scale=scale),
        out_shape=(out_shape, out_shape),
        grid_spec=pltpu.PrefetchScalarGridSpec(
            num_scalar_prefetch=2,
            grid=(blocks, slots),
            in_specs=in_specs,
            out_specs=(out_spec, out_spec),
        ),
        compiler_params=pltpu.CompilerParams(dimension_semantics=("arbitrary", "arbitrary")),
        cost_estimate=cost,
    )(ids, cnt, *operands)


def local(sources, log_a, targets, g_old, log_b, tile_ids, live_count):
    tiles_own, width, depth = targets.shape
    rows = sources.shape[0]
    slots_per = tile_ids.shape[2]
    groups = tile_ids.shape[1]
    me = lax.axis_index("src")
    scale = 1.0 / (math.sqrt(depth) * EPSILON)

    meta = jnp.concatenate([tile_ids[0].reshape(-1), live_count[0].reshape(-1)])
    meta_rows = jnp.zeros((16, depth), jnp.bfloat16).at[0, : meta.shape[0]].set(
        meta.astype(jnp.bfloat16)
    )
    packed = jnp.concatenate([sources, meta_rows], axis=0)
    x_all = lax.all_gather(packed, "src")
    meta_all = x_all[:, rows, : meta.shape[0]].astype(jnp.int32)
    blocks = x_all.shape[0]
    ids_all = meta_all[:, : groups * slots_per].reshape(blocks, groups, slots_per)
    cnt_all = meta_all[:, groups * slots_per :]
    my_ids = jnp.clip(lax.dynamic_index_in_dim(ids_all, me, 1, False) - me * tiles_own, 0, tiles_own - 1)
    my_cnt = lax.dynamic_index_in_dim(cnt_all, me, 1, False)

    g_col = (g_old.astype(jnp.float32) / EPSILON)[:, :, None]
    row_top, row_total = pass_call(
        row_kernel, my_ids, my_cnt, g_col, x_all, targets, rows, blocks, scale, True
    )
    stats = jnp.concatenate(
        [row_top.reshape(blocks, rows), row_total.reshape(blocks, rows), log_a[None]], axis=0
    )
    stats_all = lax.all_gather(stats, "src")
    tops = stats_all[:, :blocks]
    top = jnp.max(tops, axis=0)
    total = jnp.sum(stats_all[:, blocks : 2 * blocks] * jnp.exp(tops - top[None]), axis=0)
    log_a_all = stats_all[:, 2 * blocks]
    f_all = EPSILON * log_a_all - EPSILON * (top + jnp.log(total))
    f_new = lax.dynamic_index_in_dim(f_all, me, 0, False)

    f_col = (f_all / EPSILON)[:, :, None]
    tile_top, tile_total = pass_call(
        col_kernel, my_ids, my_cnt, f_col, x_all, targets, rows, tiles_own, scale, False
    )
    col = jnp.concatenate([tile_top.reshape(tiles_own, width), tile_total.reshape(tiles_own, width)])
    col_all = lax.all_gather(col, "loop")
    tops = col_all[:, :tiles_own]
    all_top = jnp.max(tops, axis=0)
    all_total = jnp.sum(col_all[:, tiles_own:] * jnp.exp(tops - all_top[None]), axis=0)
    g_new = EPSILON * log_b - EPSILON * (all_top + jnp.log(all_total))
    return (f_new, g_new)


def solution(mesh):
    return jax.shard_map(
        local,
        mesh=mesh,
        in_specs=(
            P(("src", "loop"), None),
            P(("src", "loop")),
            P("src", None, None),
            P("src", None),
            P("src", None),
            P(("src", "loop"), None, None),
            P(("src", "loop"), None),
        ),
        out_specs=(P(("src", "loop")), P("src", None)),
        check_vma=False,
    )
```

```python
import math

import jax
import jax.numpy as jnp
from jax import lax
from jax.experimental import pallas as pl
from jax.experimental.pallas import tpu as pltpu
from jax.sharding import PartitionSpec as P

EPSILON = 0.1
VERY_LOW = -1e30
NT_DIMS = (((1,), (1,)), ((), ()))


def row_kernel(ids_ref, cnt_ref, g_ref, t_ref, x_ref, top_ref, tot_ref, k_ref, *, scale):
    s = pl.program_id(0)
    c = pl.program_id(1)

    @pl.when(c == 0)
    def _():
        top_ref[...] = jnp.full(top_ref.shape, VERY_LOW, jnp.float32)
        tot_ref[...] = jnp.zeros(tot_ref.shape, jnp.float32)

    @pl.when(c < cnt_ref[s])
    def _():
        kt = lax.dot_general(t_ref[...], x_ref[...], NT_DIMS, preferred_element_type=jnp.float32)
        kt = kt * scale
        k_ref[...] = kt
        logits = g_ref[...] + kt
        old = top_ref[...]
        new = jnp.maximum(old, jnp.max(logits, axis=0, keepdims=True))
        tot_ref[...] = tot_ref[...] * jnp.exp(old - new) + jnp.sum(
            jnp.exp(logits - new), axis=0, keepdims=True
        )
        top_ref[...] = new


def col_kernel(ids_ref, cnt_ref, f_ref, k_ref, top_ref, tot_ref):
    s = pl.program_id(0)
    c = pl.program_id(1)

    @pl.when((s == 0) & (c == 0))
    def _():
        top_ref[...] = jnp.full(top_ref.shape, VERY_LOW, jnp.float32)
        tot_ref[...] = jnp.zeros(tot_ref.shape, jnp.float32)

    @pl.when(c < cnt_ref[s])
    def _():
        logits = k_ref[...] + f_ref[...]
        t = ids_ref[s, c]
        old = top_ref[t]
        new = jnp.maximum(old, jnp.max(logits, axis=1, keepdims=True))
        tot_ref[t] = tot_ref[t] * jnp.exp(old - new) + jnp.sum(
            jnp.exp(logits - new), axis=1, keepdims=True
        )
        top_ref[t] = new


def pick_tile(s, c, ids_ref, cnt_ref):
    live = c < cnt_ref[s]
    return (jnp.where(live, ids_ref[s, c], ids_ref[s, 0]), 0, 0)


def pick_slot(s, c, ids_ref, cnt_ref):
    return (s, jnp.where(c < cnt_ref[s], c, 0), 0, 0)


def row_call(ids, cnt, g_col, targets, x_all, rows, scale):
    blocks, depth = x_all.shape[0], x_all.shape[2]
    slots = ids.shape[1]
    width = targets.shape[1]
    stat_spec = pl.BlockSpec((None, 1, rows), lambda s, c, ids_ref, cnt_ref: (s, 0, 0))
    stat_shape = jax.ShapeDtypeStruct((blocks, 1, rows), jnp.float32)
    cost = pl.CostEstimate(
        flops=2 * blocks * slots * rows * width * depth,
        transcendentals=blocks * slots * rows * width,
        bytes_accessed=2 * (x_all.size + blocks * slots * width * depth)
        + 4 * blocks * slots * rows * width,
    )
    return pl.pallas_call(
        lambda *refs: row_kernel(*refs, scale=scale),
        out_shape=(
            stat_shape,
            stat_shape,
            jax.ShapeDtypeStruct((blocks, slots, width, rows), jnp.float32),
        ),
        grid_spec=pltpu.PrefetchScalarGridSpec(
            num_scalar_prefetch=2,
            grid=(blocks, slots),
            in_specs=[
                pl.BlockSpec((None, width, 1), pick_tile),
                pl.BlockSpec((None, width, depth), pick_tile),
                pl.BlockSpec((None, rows, depth), lambda s, c, ids_ref, cnt_ref: (s, 0, 0)),
            ],
            out_specs=(stat_spec, stat_spec, pl.BlockSpec((None, None, width, rows), pick_slot)),
        ),
        compiler_params=pltpu.CompilerParams(dimension_semantics=("arbitrary", "arbitrary")),
        cost_estimate=cost,
    )(ids, cnt, g_col, targets, x_all)


def col_call(ids, cnt, f_row, k_all, tiles_own):
    blocks, slots, width, rows = k_all.shape
    acc_spec = pl.BlockSpec((tiles_own, width, 1), lambda s, c, ids_ref, cnt_ref: (0, 0, 0))
    acc_shape = jax.ShapeDtypeStruct((tiles_own, width, 1), jnp.float32)
    cost = pl.CostEstimate(
        flops=4 * blocks * slots * rows * width,
        transcendentals=blocks * slots * rows * width,
        bytes_accessed=4 * blocks * slots * rows * width,
    )
    return pl.pallas_call(
        col_kernel,
        out_shape=(acc_shape, acc_shape),
        grid_spec=pltpu.PrefetchScalarGridSpec(
            num_scalar_prefetch=2,
            grid=(blocks, slots),
            in_specs=[
                pl.BlockSpec((None, 1, rows), lambda s, c, ids_ref, cnt_ref: (s, 0, 0)),
                pl.BlockSpec((None, None, width, rows), pick_slot),
            ],
            out_specs=(acc_spec, acc_spec),
        ),
        compiler_params=pltpu.CompilerParams(dimension_semantics=("arbitrary", "arbitrary")),
        cost_estimate=cost,
    )(ids, cnt, f_row, k_all)


def local(sources, log_a, targets, g_old, log_b, tile_ids, live_count):
    tiles_own, width, depth = targets.shape
    rows = sources.shape[0]
    slots_per = tile_ids.shape[2]
    groups = tile_ids.shape[1]
    me = lax.axis_index("src")
    scale = 1.0 / (math.sqrt(depth) * EPSILON)

    meta = jnp.concatenate([tile_ids[0].reshape(-1), live_count[0].reshape(-1)])
    meta_rows = jnp.zeros((16, depth), jnp.bfloat16).at[0, : meta.shape[0]].set(
        meta.astype(jnp.bfloat16)
    )
    packed = jnp.concatenate([sources, meta_rows], axis=0)
    x_all = lax.all_gather(packed, "src")
    meta_all = x_all[:, rows, : meta.shape[0]].astype(jnp.int32)
    blocks = x_all.shape[0]
    ids_all = meta_all[:, : groups * slots_per].reshape(blocks, groups, slots_per)
    cnt_all = meta_all[:, groups * slots_per :]
    my_ids = jnp.clip(lax.dynamic_index_in_dim(ids_all, me, 1, False) - me * tiles_own, 0, tiles_own - 1)
    my_cnt = lax.dynamic_index_in_dim(cnt_all, me, 1, False)

    g_col = (g_old.astype(jnp.float32) / EPSILON)[:, :, None]
    row_top, row_total, k_all = row_call(my_ids, my_cnt, g_col, targets, x_all, rows, scale)
    stats = jnp.concatenate(
        [row_top.reshape(blocks, rows), row_total.reshape(blocks, rows), log_a[None]], axis=0
    )
    stats_all = lax.all_gather(stats, "src")
    tops = stats_all[:, :blocks]
    top = jnp.max(tops, axis=0)
    total = jnp.sum(stats_all[:, blocks : 2 * blocks] * jnp.exp(tops - top[None]), axis=0)
    log_a_all = stats_all[:, 2 * blocks]
    f_all = EPSILON * log_a_all - EPSILON * (top + jnp.log(total))
    f_new = lax.dynamic_index_in_dim(f_all, me, 0, False)

    f_row = (f_all / EPSILON)[:, None, :]
    tile_top, tile_total = col_call(my_ids, my_cnt, f_row, k_all, tiles_own)
    col = jnp.concatenate([tile_top.reshape(tiles_own, width), tile_total.reshape(tiles_own, width)])
    loop_size = lax.axis_size("loop")
    col_all = lax.all_to_all(
        jnp.broadcast_to(col[None], (loop_size,) + col.shape), "loop", 0, 0, tiled=True
    )
    tops = col_all[:, :tiles_own]
    all_top = jnp.max(tops, axis=0)
    all_total = jnp.sum(col_all[:, tiles_own:] * jnp.exp(tops - all_top[None]), axis=0)
    g_new = EPSILON * log_b - EPSILON * (all_top + jnp.log(all_total))
    return (f_new, g_new)


def solution(mesh):
    return jax.shard_map(
        local,
        mesh=mesh,
        in_specs=(
            P(("src", "loop"), None),
            P(("src", "loop")),
            P("src", None, None),
            P("src", None),
            P("src", None),
            P(("src", "loop"), None, None),
            P(("src", "loop"), None),
        ),
        out_specs=(P(("src", "loop")), P("src", None)),
        check_vma=False,
    )
```

```python
import math

import jax
import jax.numpy as jnp
from jax import lax
from jax.experimental import pallas as pl
from jax.experimental.pallas import tpu as pltpu
from jax.sharding import PartitionSpec as P

EPSILON = 0.1
VERY_LOW = -1e30
NT_DIMS = (((1,), (1,)), ((), ()))


def row_kernel(ids_ref, cnt_ref, g_ref, t_ref, x_ref, top_ref, tot_ref, k_ref, *, scale):
    s = pl.program_id(0)
    c = pl.program_id(1)

    @pl.when(c == 0)
    def _():
        top_ref[...] = jnp.full(top_ref.shape, VERY_LOW, jnp.float32)
        tot_ref[...] = jnp.zeros(tot_ref.shape, jnp.float32)

    @pl.when(c < cnt_ref[s])
    def _():
        kt = lax.dot_general(t_ref[...], x_ref[...], NT_DIMS, preferred_element_type=jnp.float32)
        kt = kt * scale
        k_ref[...] = kt
        logits = g_ref[...] + kt
        old = top_ref[...]
        new = jnp.maximum(old, jnp.max(logits, axis=0, keepdims=True))
        tot_ref[...] = tot_ref[...] * jnp.exp(old - new) + jnp.sum(
            jnp.exp(logits - new), axis=0, keepdims=True
        )
        top_ref[...] = new


def col_kernel(ids_ref, cnt_ref, f_ref, k_ref, top_ref, tot_ref):
    s = pl.program_id(0)
    c = pl.program_id(1)

    @pl.when((s == 0) & (c == 0))
    def _():
        top_ref[...] = jnp.full(top_ref.shape, VERY_LOW, jnp.float32)
        tot_ref[...] = jnp.zeros(tot_ref.shape, jnp.float32)

    @pl.when(c < cnt_ref[s])
    def _():
        logits = k_ref[...] + f_ref[...]
        t = ids_ref[s, c]
        old = top_ref[t]
        new = jnp.maximum(old, jnp.max(logits, axis=1, keepdims=True))
        tot_ref[t] = tot_ref[t] * jnp.exp(old - new) + jnp.sum(
            jnp.exp(logits - new), axis=1, keepdims=True
        )
        top_ref[t] = new


def pick_tile(s, c, ids_ref, cnt_ref):
    live = c < cnt_ref[s]
    return (jnp.where(live, ids_ref[s, c], ids_ref[s, 0]), 0, 0)


def pick_slot(s, c, ids_ref, cnt_ref):
    return (s, jnp.where(c < cnt_ref[s], c, 0), 0, 0)


def row_call(ids, cnt, g_col, targets, x_all, rows, scale):
    blocks, depth = x_all.shape[0], x_all.shape[2]
    slots = ids.shape[1]
    width = targets.shape[1]
    stat_spec = pl.BlockSpec((None, 1, rows), lambda s, c, ids_ref, cnt_ref: (s, 0, 0))
    stat_shape = jax.ShapeDtypeStruct((blocks, 1, rows), jnp.float32)
    cost = pl.CostEstimate(
        flops=2 * blocks * slots * rows * width * depth,
        transcendentals=blocks * slots * rows * width,
        bytes_accessed=2 * (x_all.size + blocks * slots * width * depth)
        + 4 * blocks * slots * rows * width,
    )
    return pl.pallas_call(
        lambda *refs: row_kernel(*refs, scale=scale),
        out_shape=(
            stat_shape,
            stat_shape,
            jax.ShapeDtypeStruct((blocks, slots, width, rows), jnp.float32),
        ),
        grid_spec=pltpu.PrefetchScalarGridSpec(
            num_scalar_prefetch=2,
            grid=(blocks, slots),
            in_specs=[
                pl.BlockSpec((None, width, 1), pick_tile),
                pl.BlockSpec((None, width, depth), pick_tile),
                pl.BlockSpec((None, rows, depth), lambda s, c, ids_ref, cnt_ref: (s, 0, 0)),
            ],
            out_specs=(stat_spec, stat_spec, pl.BlockSpec((None, None, width, rows), pick_slot)),
        ),
        compiler_params=pltpu.CompilerParams(dimension_semantics=("arbitrary", "arbitrary")),
        cost_estimate=cost,
    )(ids, cnt, g_col, targets, x_all)


def col_call(ids, cnt, f_row, k_all, tiles_own):
    blocks, slots, width, rows = k_all.shape
    acc_spec = pl.BlockSpec((tiles_own, width, 1), lambda s, c, ids_ref, cnt_ref: (0, 0, 0))
    acc_shape = jax.ShapeDtypeStruct((tiles_own, width, 1), jnp.float32)
    cost = pl.CostEstimate(
        flops=4 * blocks * slots * rows * width,
        transcendentals=blocks * slots * rows * width,
        bytes_accessed=4 * blocks * slots * rows * width,
    )
    return pl.pallas_call(
        col_kernel,
        out_shape=(acc_shape, acc_shape),
        grid_spec=pltpu.PrefetchScalarGridSpec(
            num_scalar_prefetch=2,
            grid=(blocks, slots),
            in_specs=[
                pl.BlockSpec((None, 1, rows), lambda s, c, ids_ref, cnt_ref: (s, 0, 0)),
                pl.BlockSpec((None, None, width, rows), pick_slot),
            ],
            out_specs=(acc_spec, acc_spec),
        ),
        compiler_params=pltpu.CompilerParams(dimension_semantics=("arbitrary", "arbitrary")),
        cost_estimate=cost,
    )(ids, cnt, f_row, k_all)


def local(sources, log_a, targets, g_old, log_b, tile_ids, live_count):
    tiles_own, width, depth = targets.shape
    rows = sources.shape[0]
    slots_per = tile_ids.shape[2]
    groups = tile_ids.shape[1]
    me = lax.axis_index("src")
    scale = 1.0 / (math.sqrt(depth) * EPSILON)

    meta = jnp.concatenate([tile_ids[0].reshape(-1), live_count[0].reshape(-1)])
    meta_rows = jnp.zeros((16, depth), jnp.bfloat16).at[0, : meta.shape[0]].set(
        meta.astype(jnp.bfloat16)
    )
    packed = jnp.concatenate([sources, meta_rows], axis=0)
    x_all = lax.all_gather(packed, "src")
    meta_all = x_all[:, rows, : meta.shape[0]].astype(jnp.int32)
    blocks = x_all.shape[0]
    ids_all = meta_all[:, : groups * slots_per].reshape(blocks, groups, slots_per)
    cnt_all = meta_all[:, groups * slots_per :]
    my_ids = jnp.clip(lax.dynamic_index_in_dim(ids_all, me, 1, False) - me * tiles_own, 0, tiles_own - 1)
    my_cnt = lax.dynamic_index_in_dim(cnt_all, me, 1, False)

    g_col = (g_old.astype(jnp.float32) / EPSILON)[:, :, None]
    row_top, row_total, k_all = row_call(my_ids, my_cnt, g_col, targets, x_all, rows, scale)
    stats = jnp.concatenate(
        [row_top.reshape(blocks, rows), row_total.reshape(blocks, rows), log_a[None]], axis=0
    )
    stats_all = lax.all_to_all(
        jnp.broadcast_to(stats[None], (blocks,) + stats.shape), "src", 0, 0, tiled=True
    )
    tops = stats_all[:, :blocks]
    top = jnp.max(tops, axis=0)
    total = jnp.sum(stats_all[:, blocks : 2 * blocks] * jnp.exp(tops - top[None]), axis=0)
    log_a_all = stats_all[:, 2 * blocks]
    f_all = EPSILON * log_a_all - EPSILON * (top + jnp.log(total))
    f_new = lax.dynamic_index_in_dim(f_all, me, 0, False)

    f_row = (f_all / EPSILON)[:, None, :]
    tile_top, tile_total = col_call(my_ids, my_cnt, f_row, k_all, tiles_own)
    col = jnp.concatenate([tile_top.reshape(tiles_own, width), tile_total.reshape(tiles_own, width)])
    loop_size = lax.axis_size("loop")
    col_all = lax.all_to_all(
        jnp.broadcast_to(col[None], (loop_size,) + col.shape), "loop", 0, 0, tiled=True
    )
    tops = col_all[:, :tiles_own]
    all_top = jnp.max(tops, axis=0)
    all_total = jnp.sum(col_all[:, tiles_own:] * jnp.exp(tops - all_top[None]), axis=0)
    g_new = EPSILON * log_b - EPSILON * (all_top + jnp.log(all_total))
    return (f_new, g_new)


def solution(mesh):
    return jax.shard_map(
        local,
        mesh=mesh,
        in_specs=(
            P(("src", "loop"), None),
            P(("src", "loop")),
            P("src", None, None),
            P("src", None),
            P("src", None),
            P(("src", "loop"), None, None),
            P(("src", "loop"), None),
        ),
        out_specs=(P(("src", "loop")), P("src", None)),
        check_vma=False,
    )
```

```python
import math

import jax
import jax.numpy as jnp
from jax import lax
from jax.experimental import pallas as pl
from jax.experimental.pallas import tpu as pltpu
from jax.sharding import PartitionSpec as P

EPSILON = 0.1
VERY_LOW = -1e30
NT_DIMS = (((1,), (1,)), ((), ()))


def row_kernel(ids_ref, cnt_ref, g_ref, t_ref, x_ref, top_ref, tot_ref, k_ref, *, scale):
    s = pl.program_id(0)
    c = pl.program_id(1)

    @pl.when(c == 0)
    def _():
        top_ref[...] = jnp.full(top_ref.shape, VERY_LOW, jnp.float32)
        tot_ref[...] = jnp.zeros(tot_ref.shape, jnp.float32)

    @pl.when(c < cnt_ref[s])
    def _():
        kt = lax.dot_general(t_ref[...], x_ref[...], NT_DIMS, preferred_element_type=jnp.float32)
        kt = kt * scale
        k_ref[...] = kt
        logits = g_ref[...] + kt
        old = top_ref[...]
        new = jnp.maximum(old, jnp.max(logits, axis=0, keepdims=True))
        tot_ref[...] = tot_ref[...] * jnp.exp(old - new) + jnp.sum(
            jnp.exp(logits - new), axis=0, keepdims=True
        )
        top_ref[...] = new


def col_kernel(ids_ref, cnt_ref, *refs):
    parts = (len(refs) - 2) // 2
    f_refs, k_refs = refs[:parts], refs[parts : 2 * parts]
    top_ref, tot_ref = refs[2 * parts :]
    s = pl.program_id(0)
    c = pl.program_id(1)

    @pl.when((s == 0) & (c == 0))
    def _():
        top_ref[...] = jnp.full(top_ref.shape, VERY_LOW, jnp.float32)
        tot_ref[...] = jnp.zeros(tot_ref.shape, jnp.float32)

    @pl.when(c < cnt_ref[s])
    def _():
        logits = [k_ref[...] + f_ref[...] for f_ref, k_ref in zip(f_refs, k_refs)]
        t = ids_ref[s, c]
        old = top_ref[t]
        new = old
        for part in logits:
            new = jnp.maximum(new, jnp.max(part, axis=1, keepdims=True))
        acc = tot_ref[t] * jnp.exp(old - new)
        for part in logits:
            acc = acc + jnp.sum(jnp.exp(part - new), axis=1, keepdims=True)
        tot_ref[t] = acc
        top_ref[t] = new


def pick_tile(s, c, ids_ref, cnt_ref):
    live = c < cnt_ref[s]
    return (jnp.where(live, ids_ref[s, c], ids_ref[s, 0]), 0, 0)


def pick_slot(s, c, ids_ref, cnt_ref):
    return (s, jnp.where(c < cnt_ref[s], c, 0), 0, 0)


def row_call(ids, cnt, g_col, targets, x_all, rows, scale):
    blocks, depth = x_all.shape[0], x_all.shape[2]
    slots = ids.shape[1]
    width = targets.shape[1]
    stat_spec = pl.BlockSpec((None, 1, rows), lambda s, c, ids_ref, cnt_ref: (s, 0, 0))
    stat_shape = jax.ShapeDtypeStruct((blocks, 1, rows), jnp.float32)
    cost = pl.CostEstimate(
        flops=2 * blocks * slots * rows * width * depth,
        transcendentals=blocks * slots * rows * width,
        bytes_accessed=2 * (x_all.size + blocks * slots * width * depth)
        + 4 * blocks * slots * rows * width,
    )
    return pl.pallas_call(
        lambda *refs: row_kernel(*refs, scale=scale),
        out_shape=(
            stat_shape,
            stat_shape,
            jax.ShapeDtypeStruct((blocks, slots, width, rows), jnp.float32),
        ),
        grid_spec=pltpu.PrefetchScalarGridSpec(
            num_scalar_prefetch=2,
            grid=(blocks, slots),
            in_specs=[
                pl.BlockSpec((None, width, 1), pick_tile),
                pl.BlockSpec((None, width, depth), pick_tile),
                pl.BlockSpec((None, rows, depth), lambda s, c, ids_ref, cnt_ref: (s, 0, 0)),
            ],
            out_specs=(stat_spec, stat_spec, pl.BlockSpec((None, None, width, rows), pick_slot)),
        ),
        compiler_params=pltpu.CompilerParams(dimension_semantics=("arbitrary", "arbitrary")),
        cost_estimate=cost,
    )(ids, cnt, g_col, targets, x_all)


def col_call(ids, cnt, f_rows, k_parts, tiles_own):
    blocks, slots, width, part_rows = k_parts[0].shape
    rows = part_rows * len(k_parts)
    acc_spec = pl.BlockSpec((tiles_own, width, 1), lambda s, c, ids_ref, cnt_ref: (0, 0, 0))
    acc_shape = jax.ShapeDtypeStruct((tiles_own, width, 1), jnp.float32)
    cost = pl.CostEstimate(
        flops=4 * blocks * slots * rows * width,
        transcendentals=blocks * slots * rows * width,
        bytes_accessed=4 * blocks * slots * rows * width,
    )
    f_spec = pl.BlockSpec((None, 1, part_rows), lambda s, c, ids_ref, cnt_ref: (s, 0, 0))
    k_spec = pl.BlockSpec((None, None, width, part_rows), pick_slot)
    return pl.pallas_call(
        col_kernel,
        out_shape=(acc_shape, acc_shape),
        grid_spec=pltpu.PrefetchScalarGridSpec(
            num_scalar_prefetch=2,
            grid=(blocks, slots),
            in_specs=[f_spec] * len(f_rows) + [k_spec] * len(k_parts),
            out_specs=(acc_spec, acc_spec),
        ),
        compiler_params=pltpu.CompilerParams(dimension_semantics=("arbitrary", "arbitrary")),
        cost_estimate=cost,
    )(ids, cnt, *f_rows, *k_parts)


def local(sources, log_a, targets, g_old, log_b, tile_ids, live_count):
    tiles_own, width, depth = targets.shape
    rows = sources.shape[0]
    slots_per = tile_ids.shape[2]
    groups = tile_ids.shape[1]
    me = lax.axis_index("src")
    scale = 1.0 / (math.sqrt(depth) * EPSILON)

    meta = jnp.concatenate([tile_ids[0].reshape(-1), live_count[0].reshape(-1)])
    meta_rows = jnp.zeros((16, depth), jnp.bfloat16).at[0, : meta.shape[0]].set(
        meta.astype(jnp.bfloat16)
    )
    half = rows // 2
    x_first = lax.all_gather(jnp.concatenate([sources[:half], meta_rows], axis=0), "src")
    x_second = lax.all_gather(sources[half:], "src")
    meta_all = x_first[:, half, : meta.shape[0]].astype(jnp.int32)
    blocks = x_first.shape[0]
    ids_all = meta_all[:, : groups * slots_per].reshape(blocks, groups, slots_per)
    cnt_all = meta_all[:, groups * slots_per :]
    my_ids = jnp.clip(lax.dynamic_index_in_dim(ids_all, me, 1, False) - me * tiles_own, 0, tiles_own - 1)
    my_cnt = lax.dynamic_index_in_dim(cnt_all, me, 1, False)

    g_col = (g_old.astype(jnp.float32) / EPSILON)[:, :, None]
    top_a, total_a, k_a = row_call(my_ids, my_cnt, g_col, targets, x_first, half, scale)
    top_b, total_b, k_b = row_call(my_ids, my_cnt, g_col, targets, x_second, half, scale)
    row_top = jnp.concatenate([top_a, top_b], axis=2).reshape(blocks, rows)
    row_total = jnp.concatenate([total_a, total_b], axis=2).reshape(blocks, rows)
    stats = jnp.concatenate([row_top, row_total, log_a[None]], axis=0)
    stats_all = lax.all_to_all(
        jnp.broadcast_to(stats[None], (blocks,) + stats.shape), "src", 0, 0, tiled=True
    )
    tops = stats_all[:, :blocks]
    top = jnp.max(tops, axis=0)
    total = jnp.sum(stats_all[:, blocks : 2 * blocks] * jnp.exp(tops - top[None]), axis=0)
    log_a_all = stats_all[:, 2 * blocks]
    f_all = EPSILON * log_a_all - EPSILON * (top + jnp.log(total))
    f_new = lax.dynamic_index_in_dim(f_all, me, 0, False)

    f_row = (f_all / EPSILON)[:, None, :]
    f_rows = (f_row[:, :, :half], f_row[:, :, half:])
    tile_top, tile_total = col_call(my_ids, my_cnt, f_rows, (k_a, k_b), tiles_own)
    col = jnp.concatenate([tile_top.reshape(tiles_own, width), tile_total.reshape(tiles_own, width)])
    loop_size = lax.axis_size("loop")
    col_all = lax.all_to_all(
        jnp.broadcast_to(col[None], (loop_size,) + col.shape), "loop", 0, 0, tiled=True
    )
    tops = col_all[:, :tiles_own]
    all_top = jnp.max(tops, axis=0)
    all_total = jnp.sum(col_all[:, tiles_own:] * jnp.exp(tops - all_top[None]), axis=0)
    g_new = EPSILON * log_b - EPSILON * (all_top + jnp.log(all_total))
    return (f_new, g_new)


def solution(mesh):
    return jax.shard_map(
        local,
        mesh=mesh,
        in_specs=(
            P(("src", "loop"), None),
            P(("src", "loop")),
            P("src", None, None),
            P("src", None),
            P("src", None),
            P(("src", "loop"), None, None),
            P(("src", "loop"), None),
        ),
        out_specs=(P(("src", "loop")), P("src", None)),
        check_vma=False,
    )
```

```python
import math

import jax
import jax.numpy as jnp
from jax import lax
from jax.experimental import pallas as pl
from jax.experimental.pallas import tpu as pltpu
from jax.sharding import PartitionSpec as P

EPSILON = 0.1
VERY_LOW = -1e30
NT_DIMS = (((1,), (1,)), ((), ()))


def load_all(t_hbm, x_hbm, t_vmem, x_vmem, t_sem, x_sem, window):
    tiles, blocks = t_vmem.shape[0], x_vmem.shape[0]
    rows = x_vmem.shape[1]

    def x_copy(s):
        return pltpu.make_async_copy(x_hbm.at[s, pl.ds(0, rows)], x_vmem.at[s], x_sem.at[s])

    def t_copy(t):
        return pltpu.make_async_copy(t_hbm.at[t], t_vmem.at[t], t_sem.at[t])

    for t in range(tiles):
        t_copy(t).start()
    for s in range(min(window, blocks)):
        x_copy(s).start()
    for t in range(tiles):
        t_copy(t).wait()

    def arrive(s):
        x_copy(s).wait()

        @pl.when(s + window < blocks)
        def _():
            x_copy(jnp.minimum(s + window, blocks - 1)).start()

    return arrive


def row_kernel(ids_ref, cnt_ref, g_ref, t_hbm, x_hbm, top_ref, tot_ref, t_vmem, x_vmem, t_sem, x_sem, *, scale, slots, window):
    arrive = load_all(t_hbm, x_hbm, t_vmem, x_vmem, t_sem, x_sem, window)

    def step(s, carry):
        arrive(s)
        top_ref[s] = jnp.full(top_ref.shape[1:], VERY_LOW, jnp.float32)
        tot_ref[s] = jnp.zeros(tot_ref.shape[1:], jnp.float32)
        for c in range(slots):

            @pl.when(c < cnt_ref[s])
            def _():
                t = ids_ref[s * slots + c]
                kt = lax.dot_general(t_vmem[t], x_vmem[s], NT_DIMS, preferred_element_type=jnp.float32)
                logits = g_ref[t] + kt * scale
                old = top_ref[s]
                new = jnp.maximum(old, jnp.max(logits, axis=0, keepdims=True))
                tot_ref[s] = tot_ref[s] * jnp.exp(old - new) + jnp.sum(
                    jnp.exp(logits - new), axis=0, keepdims=True
                )
                top_ref[s] = new

        return carry

    lax.fori_loop(0, x_vmem.shape[0], step, 0)


def col_kernel(ids_ref, cnt_ref, f_ref, t_hbm, x_hbm, top_ref, tot_ref, t_vmem, x_vmem, t_sem, x_sem, *, scale, slots, window):
    arrive = load_all(t_hbm, x_hbm, t_vmem, x_vmem, t_sem, x_sem, window)
    top_ref[...] = jnp.full(top_ref.shape, VERY_LOW, jnp.float32)
    tot_ref[...] = jnp.zeros(tot_ref.shape, jnp.float32)

    def step(s, carry):
        arrive(s)
        for c in range(slots):

            @pl.when(c < cnt_ref[s])
            def _():
                t = ids_ref[s * slots + c]
                kt = lax.dot_general(t_vmem[t], x_vmem[s], NT_DIMS, preferred_element_type=jnp.float32)
                logits = kt * scale + f_ref[s]
                old = top_ref[t]
                new = jnp.maximum(old, jnp.max(logits, axis=1, keepdims=True))
                tot_ref[t] = tot_ref[t] * jnp.exp(old - new) + jnp.sum(
                    jnp.exp(logits - new), axis=1, keepdims=True
                )
                top_ref[t] = new

        return carry

    lax.fori_loop(0, x_vmem.shape[0], step, 0)


def resident_call(body, ids, cnt, side, targets, x_all, rows, out_shape, scale):
    tiles, width, depth = targets.shape
    blocks = x_all.shape[0]
    slots = ids.shape[1]
    smem = pl.BlockSpec(memory_space=pltpu.SMEM)
    vmem = pl.BlockSpec(memory_space=pltpu.VMEM)
    hbm = pl.BlockSpec(memory_space=pl.ANY)
    cost = pl.CostEstimate(
        flops=2 * blocks * slots * rows * width * depth,
        transcendentals=blocks * slots * rows * width,
        bytes_accessed=2 * (targets.size + blocks * rows * depth),
    )
    kernel = lambda *refs: body(*refs, scale=scale, slots=slots, window=4)
    return pl.pallas_call(
        kernel,
        out_shape=(out_shape, out_shape),
        in_specs=[smem, smem, vmem, hbm, hbm],
        out_specs=(vmem, vmem),
        scratch_shapes=[
            pltpu.VMEM((tiles, width, depth), targets.dtype),
            pltpu.VMEM((blocks, rows, depth), x_all.dtype),
            pltpu.SemaphoreType.DMA((tiles,)),
            pltpu.SemaphoreType.DMA((blocks,)),
        ],
        compiler_params=pltpu.CompilerParams(vmem_limit_bytes=56 * 1024 * 1024),
        cost_estimate=cost,
    )(ids.reshape(-1), cnt, side, targets, x_all)


def local(sources, log_a, targets, g_old, log_b, tile_ids, live_count):
    tiles_own, width, depth = targets.shape
    rows = sources.shape[0]
    slots_per = tile_ids.shape[2]
    groups = tile_ids.shape[1]
    me = lax.axis_index("src")
    scale = 1.0 / (math.sqrt(depth) * EPSILON)

    meta = jnp.concatenate([tile_ids[0].reshape(-1), live_count[0].reshape(-1)])
    meta_rows = jnp.zeros((16, depth), jnp.bfloat16).at[0, : meta.shape[0]].set(
        meta.astype(jnp.bfloat16)
    )
    packed = jnp.concatenate([sources, meta_rows], axis=0)
    x_all = lax.all_gather(packed, "src")
    meta_all = x_all[:, rows, : meta.shape[0]].astype(jnp.int32)
    blocks = x_all.shape[0]
    ids_all = meta_all[:, : groups * slots_per].reshape(blocks, groups, slots_per)
    cnt_all = meta_all[:, groups * slots_per :]
    my_ids = jnp.clip(lax.dynamic_index_in_dim(ids_all, me, 1, False) - me * tiles_own, 0, tiles_own - 1)
    my_cnt = lax.dynamic_index_in_dim(cnt_all, me, 1, False)

    g_col = (g_old.astype(jnp.float32) / EPSILON)[:, :, None]
    row_top, row_total = resident_call(
        row_kernel, my_ids, my_cnt, g_col, targets, x_all, rows,
        jax.ShapeDtypeStruct((blocks, 1, rows), jnp.float32), scale,
    )
    stats = jnp.concatenate(
        [row_top.reshape(blocks, rows), row_total.reshape(blocks, rows), log_a[None]], axis=0
    )
    stats_all = lax.all_to_all(
        jnp.broadcast_to(stats[None], (blocks,) + stats.shape), "src", 0, 0, tiled=True
    )
    tops = stats_all[:, :blocks]
    top = jnp.max(tops, axis=0)
    total = jnp.sum(stats_all[:, blocks : 2 * blocks] * jnp.exp(tops - top[None]), axis=0)
    log_a_all = stats_all[:, 2 * blocks]
    f_all = EPSILON * log_a_all - EPSILON * (top + jnp.log(total))
    f_new = lax.dynamic_index_in_dim(f_all, me, 0, False)

    f_row = (f_all / EPSILON)[:, None, :]
    tile_top, tile_total = resident_call(
        col_kernel, my_ids, my_cnt, f_row, targets, x_all, rows,
        jax.ShapeDtypeStruct((tiles_own, width, 1), jnp.float32), scale,
    )
    col = jnp.concatenate([tile_top.reshape(tiles_own, width), tile_total.reshape(tiles_own, width)])
    loop_size = lax.axis_size("loop")
    col_all = lax.all_to_all(
        jnp.broadcast_to(col[None], (loop_size,) + col.shape), "loop", 0, 0, tiled=True
    )
    tops = col_all[:, :tiles_own]
    all_top = jnp.max(tops, axis=0)
    all_total = jnp.sum(col_all[:, tiles_own:] * jnp.exp(tops - all_top[None]), axis=0)
    g_new = EPSILON * log_b - EPSILON * (all_top + jnp.log(all_total))
    return (f_new, g_new)


def solution(mesh):
    return jax.shard_map(
        local,
        mesh=mesh,
        in_specs=(
            P(("src", "loop"), None),
            P(("src", "loop")),
            P("src", None, None),
            P("src", None),
            P("src", None),
            P(("src", "loop"), None, None),
            P(("src", "loop"), None),
        ),
        out_specs=(P(("src", "loop")), P("src", None)),
        check_vma=False,
    )
```

```python
import math

import jax
import jax.numpy as jnp
from jax import lax
from jax.experimental import pallas as pl
from jax.experimental.pallas import tpu as pltpu
from jax.sharding import PartitionSpec as P

EPSILON = 0.1
VERY_LOW = -1e30
NT_DIMS = (((1,), (1,)), ((), ()))


def load_all(t_hbm, x_hbm, t_vmem, x_vmem, t_sem, x_sem, window):
    tiles, blocks = t_vmem.shape[0], x_vmem.shape[0]
    rows = x_vmem.shape[1]

    def x_copy(s):
        return pltpu.make_async_copy(x_hbm.at[s, pl.ds(0, rows)], x_vmem.at[s], x_sem.at[s])

    def t_copy(t):
        return pltpu.make_async_copy(t_hbm.at[t], t_vmem.at[t], t_sem.at[t])

    for t in range(tiles):
        t_copy(t).start()
    for s in range(min(window, blocks)):
        x_copy(s).start()
    for t in range(tiles):
        t_copy(t).wait()

    def arrive(s):
        x_copy(s).wait()

        @pl.when(s + window < blocks)
        def _():
            x_copy(jnp.minimum(s + window, blocks - 1)).start()

    return arrive


def row_kernel(ids_ref, cnt_ref, g_ref, t_hbm, x_hbm, top_ref, tot_ref, t_vmem, x_vmem, t_sem, x_sem, *, scale, slots, window):
    arrive = load_all(t_hbm, x_hbm, t_vmem, x_vmem, t_sem, x_sem, window)

    def step(s, carry):
        arrive(s)
        top_ref[s] = jnp.full(top_ref.shape[1:], VERY_LOW, jnp.float32)
        tot_ref[s] = jnp.zeros(tot_ref.shape[1:], jnp.float32)
        for c in range(slots):

            @pl.when(c < cnt_ref[s])
            def _():
                t = ids_ref[s * slots + c]
                kt = lax.dot_general(t_vmem[t], x_vmem[s], NT_DIMS, preferred_element_type=jnp.float32)
                logits = g_ref[t] + kt * scale
                old = top_ref[s]
                new = jnp.maximum(old, jnp.max(logits, axis=0, keepdims=True))
                tot_ref[s] = tot_ref[s] * jnp.exp(old - new) + jnp.sum(
                    jnp.exp(logits - new), axis=0, keepdims=True
                )
                top_ref[s] = new

        return carry

    lax.fori_loop(0, x_vmem.shape[0], step, 0)


def col_kernel(ids_ref, cnt_ref, f_ref, t_hbm, x_hbm, top_ref, tot_ref, t_vmem, x_vmem, t_sem, x_sem, *, scale, slots, window):
    arrive = load_all(t_hbm, x_hbm, t_vmem, x_vmem, t_sem, x_sem, window)
    top_ref[...] = jnp.full(top_ref.shape, VERY_LOW, jnp.float32)
    tot_ref[...] = jnp.zeros(tot_ref.shape, jnp.float32)

    def step(s, carry):
        arrive(s)
        for c in range(slots):

            @pl.when(c < cnt_ref[s])
            def _():
                t = ids_ref[s * slots + c]
                k = lax.dot_general(x_vmem[s], t_vmem[t], NT_DIMS, preferred_element_type=jnp.float32)
                logits = f_ref[s] + k * scale
                old = top_ref[t]
                new = jnp.maximum(old, jnp.max(logits, axis=0, keepdims=True))
                tot_ref[t] = tot_ref[t] * jnp.exp(old - new) + jnp.sum(
                    jnp.exp(logits - new), axis=0, keepdims=True
                )
                top_ref[t] = new

        return carry

    lax.fori_loop(0, x_vmem.shape[0], step, 0)


def resident_call(body, ids, cnt, side, targets, x_all, rows, out_shape, scale):
    tiles, width, depth = targets.shape
    blocks = x_all.shape[0]
    slots = ids.shape[1]
    smem = pl.BlockSpec(memory_space=pltpu.SMEM)
    vmem = pl.BlockSpec(memory_space=pltpu.VMEM)
    hbm = pl.BlockSpec(memory_space=pl.ANY)
    cost = pl.CostEstimate(
        flops=2 * blocks * slots * rows * width * depth,
        transcendentals=blocks * slots * rows * width,
        bytes_accessed=2 * (targets.size + blocks * rows * depth),
    )
    kernel = lambda *refs: body(*refs, scale=scale, slots=slots, window=4)
    return pl.pallas_call(
        kernel,
        out_shape=(out_shape, out_shape),
        in_specs=[smem, smem, vmem, hbm, hbm],
        out_specs=(vmem, vmem),
        scratch_shapes=[
            pltpu.VMEM((tiles, width, depth), targets.dtype),
            pltpu.VMEM((blocks, rows, depth), x_all.dtype),
            pltpu.SemaphoreType.DMA((tiles,)),
            pltpu.SemaphoreType.DMA((blocks,)),
        ],
        compiler_params=pltpu.CompilerParams(vmem_limit_bytes=56 * 1024 * 1024),
        cost_estimate=cost,
    )(ids.reshape(-1), cnt, side, targets, x_all)


def local(sources, log_a, targets, g_old, log_b, tile_ids, live_count):
    tiles_own, width, depth = targets.shape
    rows = sources.shape[0]
    slots_per = tile_ids.shape[2]
    groups = tile_ids.shape[1]
    me = lax.axis_index("src")
    scale = 1.0 / (math.sqrt(depth) * EPSILON)

    meta = jnp.concatenate([tile_ids[0].reshape(-1), live_count[0].reshape(-1)])
    meta_rows = jnp.zeros((16, depth), jnp.bfloat16).at[0, : meta.shape[0]].set(
        meta.astype(jnp.bfloat16)
    )
    packed = jnp.concatenate([sources, meta_rows], axis=0)
    x_all = lax.all_gather(packed, "src")
    meta_all = x_all[:, rows, : meta.shape[0]].astype(jnp.int32)
    blocks = x_all.shape[0]
    ids_all = meta_all[:, : groups * slots_per].reshape(blocks, groups, slots_per)
    cnt_all = meta_all[:, groups * slots_per :]
    my_ids = jnp.clip(lax.dynamic_index_in_dim(ids_all, me, 1, False) - me * tiles_own, 0, tiles_own - 1)
    my_cnt = lax.dynamic_index_in_dim(cnt_all, me, 1, False)

    g_col = (g_old.astype(jnp.float32) / EPSILON)[:, :, None]
    row_top, row_total = resident_call(
        row_kernel, my_ids, my_cnt, g_col, targets, x_all, rows,
        jax.ShapeDtypeStruct((blocks, 1, rows), jnp.float32), scale,
    )
    stats = jnp.concatenate(
        [row_top.reshape(blocks, rows), row_total.reshape(blocks, rows), log_a[None]], axis=0
    )
    stats_all = lax.all_to_all(
        jnp.broadcast_to(stats[None], (blocks,) + stats.shape), "src", 0, 0, tiled=True
    )
    tops = stats_all[:, :blocks]
    top = jnp.max(tops, axis=0)
    total = jnp.sum(stats_all[:, blocks : 2 * blocks] * jnp.exp(tops - top[None]), axis=0)
    log_a_all = stats_all[:, 2 * blocks]
    f_all = EPSILON * log_a_all - EPSILON * (top + jnp.log(total))
    f_new = lax.dynamic_index_in_dim(f_all, me, 0, False)

    f_col = (f_all / EPSILON)[:, :, None]
    tile_top, tile_total = resident_call(
        col_kernel, my_ids, my_cnt, f_col, targets, x_all, rows,
        jax.ShapeDtypeStruct((tiles_own, 1, width), jnp.float32), scale,
    )
    col = jnp.concatenate([tile_top.reshape(tiles_own, width), tile_total.reshape(tiles_own, width)])
    loop_size = lax.axis_size("loop")
    col_all = lax.all_to_all(
        jnp.broadcast_to(col[None], (loop_size,) + col.shape), "loop", 0, 0, tiled=True
    )
    tops = col_all[:, :tiles_own]
    all_top = jnp.max(tops, axis=0)
    all_total = jnp.sum(col_all[:, tiles_own:] * jnp.exp(tops - all_top[None]), axis=0)
    g_new = EPSILON * log_b - EPSILON * (all_top + jnp.log(all_total))
    return (f_new, g_new)


def solution(mesh):
    return jax.shard_map(
        local,
        mesh=mesh,
        in_specs=(
            P(("src", "loop"), None),
            P(("src", "loop")),
            P("src", None, None),
            P("src", None),
            P("src", None),
            P(("src", "loop"), None, None),
            P(("src", "loop"), None),
        ),
        out_specs=(P(("src", "loop")), P("src", None)),
        check_vma=False,
    )
```

```python
import math

import jax
import jax.numpy as jnp
from jax import lax
from jax.experimental import pallas as pl
from jax.experimental.pallas import tpu as pltpu
from jax.sharding import Mesh, PartitionSpec as P


EPSILON = 0.1
VERY_LOW = -1e30
NT_DIMS = (((1,), (1,)), ((), ()))


def load_all(t_hbm, x_parts, t_vmem, x_vmem, t_sem, x_sem, window):
    tiles = t_vmem.shape[0]
    rows = x_vmem.shape[1]
    per = x_parts[0].shape[0]

    def x_copy(q, j):
        return pltpu.make_async_copy(
            x_parts[q].at[j, pl.ds(0, rows)], x_vmem.at[q * per + j], x_sem.at[q * per + j]
        )

    def t_copy(t):
        return pltpu.make_async_copy(t_hbm.at[t], t_vmem.at[t], t_sem.at[t])

    for t in range(tiles):
        t_copy(t).start()
    for q in range(len(x_parts)):
        for j in range(min(window, per)):
            x_copy(q, j).start()
    for t in range(tiles):
        t_copy(t).wait()

    def arrive(q, j):
        x_copy(q, j).wait()

        @pl.when(j + window < per)
        def _():
            x_copy(q, jnp.minimum(j + window, per - 1)).start()

    return arrive, per


def row_kernel(ids_ref, cnt_ref, g_ref, t_hbm, *refs, scale, slots, window, parts):
    x_parts = refs[:parts]
    top_ref, tot_ref, t_vmem, x_vmem, t_sem, x_sem = refs[parts:]
    arrive, per = load_all(t_hbm, x_parts, t_vmem, x_vmem, t_sem, x_sem, window)

    def step(q, j):
        arrive(q, j)
        s = q * per + j
        top_ref[s] = jnp.full(top_ref.shape[1:], VERY_LOW, jnp.float32)
        tot_ref[s] = jnp.zeros(tot_ref.shape[1:], jnp.float32)
        for c in range(slots):

            @pl.when(c < cnt_ref[s])
            def _():
                t = ids_ref[s * slots + c]
                kt = lax.dot_general(t_vmem[t], x_vmem[s], NT_DIMS, preferred_element_type=jnp.float32)
                logits = g_ref[t] + kt * scale
                old = top_ref[s]
                new = jnp.maximum(old, jnp.max(logits, axis=0, keepdims=True))
                tot_ref[s] = tot_ref[s] * jnp.exp(old - new) + jnp.sum(
                    jnp.exp(logits - new), axis=0, keepdims=True
                )
                top_ref[s] = new

    for q in range(parts):
        lax.fori_loop(0, per, lambda j, carry, q=q: (step(q, j), carry)[1], 0)


def col_kernel(ids_ref, cnt_ref, f_ref, t_hbm, *refs, scale, slots, window, parts):
    x_parts = refs[:parts]
    top_ref, tot_ref, t_vmem, x_vmem, t_sem, x_sem = refs[parts:]
    arrive, per = load_all(t_hbm, x_parts, t_vmem, x_vmem, t_sem, x_sem, window)
    top_ref[...] = jnp.full(top_ref.shape, VERY_LOW, jnp.float32)
    tot_ref[...] = jnp.zeros(tot_ref.shape, jnp.float32)

    def step(q, j):
        arrive(q, j)
        s = q * per + j
        for c in range(slots):

            @pl.when(c < cnt_ref[s])
            def _():
                t = ids_ref[s * slots + c]
                k = lax.dot_general(x_vmem[s], t_vmem[t], NT_DIMS, preferred_element_type=jnp.float32)
                logits = f_ref[s] + k * scale
                old = top_ref[t]
                new = jnp.maximum(old, jnp.max(logits, axis=0, keepdims=True))
                tot_ref[t] = tot_ref[t] * jnp.exp(old - new) + jnp.sum(
                    jnp.exp(logits - new), axis=0, keepdims=True
                )
                top_ref[t] = new

    for q in range(parts):
        lax.fori_loop(0, per, lambda j, carry, q=q: (step(q, j), carry)[1], 0)


def resident_call(body, ids, cnt, side, targets, x_parts, rows, out_shape, scale):
    tiles, width, depth = targets.shape
    blocks = sum(x.shape[0] for x in x_parts)
    slots = ids.shape[1]
    smem = pl.BlockSpec(memory_space=pltpu.SMEM)
    vmem = pl.BlockSpec(memory_space=pltpu.VMEM)
    hbm = pl.BlockSpec(memory_space=pl.ANY)
    cost = pl.CostEstimate(
        flops=2 * blocks * slots * rows * width * depth,
        transcendentals=blocks * slots * rows * width,
        bytes_accessed=2 * (targets.size + blocks * rows * depth),
    )
    kernel = lambda *refs: body(*refs, scale=scale, slots=slots, window=4, parts=len(x_parts))
    return pl.pallas_call(
        kernel,
        out_shape=(out_shape, out_shape),
        in_specs=[smem, smem, vmem, hbm] + [hbm] * len(x_parts),
        out_specs=(vmem, vmem),
        scratch_shapes=[
            pltpu.VMEM((tiles, width, depth), targets.dtype),
            pltpu.VMEM((blocks, rows, depth), x_parts[0].dtype),
            pltpu.SemaphoreType.DMA((tiles,)),
            pltpu.SemaphoreType.DMA((blocks,)),
        ],
        compiler_params=pltpu.CompilerParams(vmem_limit_bytes=56 * 1024 * 1024),
        cost_estimate=cost,
    )(ids.reshape(-1), cnt, side, targets, *x_parts)


def local_body(sources, log_a, targets, g_old, log_b, tile_ids, live_count):
    tiles_own, width, depth = targets.shape
    rows = sources.shape[0]
    slots_per = tile_ids.shape[2]
    groups = tile_ids.shape[1]
    me = lax.axis_index(SRC)
    core = lax.axis_index(CORE)
    scale = 1.0 / (math.sqrt(depth) * EPSILON)

    meta = jnp.concatenate([tile_ids[0].reshape(-1), live_count[0].reshape(-1)])
    meta_rows = jnp.zeros((16, depth), jnp.bfloat16).at[0, : meta.shape[0]].set(
        meta.astype(jnp.bfloat16)
    )
    packed = jnp.concatenate([sources, meta_rows], axis=0)
    x_own = lax.all_gather(packed, CHIPS)
    pairs = lax.axis_size(CORE)
    x_other = lax.ppermute(x_own, CORE, [(i, (i + 1) % pairs) for i in range(pairs)])
    per = x_own.shape[0]
    blocks = per * pairs
    pos = jnp.arange(per, dtype=jnp.int32) * pairs
    order = jnp.concatenate([pos + core, pos + (core + 1) % pairs])

    def listed(meta_part):
        meta_part = meta_part.astype(jnp.int32)
        ids_part = meta_part[:, : groups * slots_per].reshape(per, groups, slots_per)
        ids_part = lax.dynamic_index_in_dim(ids_part, me, 1, False) - me * tiles_own
        cnt_part = lax.dynamic_index_in_dim(meta_part[:, groups * slots_per :], me, 1, False)
        return jnp.clip(ids_part, 0, tiles_own - 1), cnt_part

    g_col = (g_old.astype(jnp.float32) / EPSILON)[:, :, None]
    stat_shape = jax.ShapeDtypeStruct((per, 1, rows), jnp.float32)
    ids_a, cnt_a = listed(x_own[:, rows, : meta.shape[0]])
    top_a, total_a = resident_call(
        row_kernel, ids_a, cnt_a, g_col, targets, [x_own], rows, stat_shape, scale
    )
    meta_b, top_a = lax.optimization_barrier((x_other[:, rows, : meta.shape[0]], top_a))
    ids_b, cnt_b = listed(meta_b)
    my_ids = jnp.concatenate([ids_a, ids_b])
    my_cnt = jnp.concatenate([cnt_a, cnt_b])
    top_b, total_b = resident_call(
        row_kernel, ids_b, cnt_b, g_col, targets, [x_other], rows, stat_shape, scale
    )
    inverse = jnp.argsort(order)
    row_top = jnp.concatenate([top_a, top_b]).reshape(blocks, rows)[inverse]
    row_total = jnp.concatenate([total_a, total_b]).reshape(blocks, rows)[inverse]
    stats = jnp.concatenate([row_top, row_total, log_a[None]], axis=0)
    stats_all = lax.all_to_all(
        jnp.broadcast_to(stats[None], (blocks,) + stats.shape), SRC, 0, 0, tiled=True
    )
    tops = stats_all[:, :blocks]
    top = jnp.max(tops, axis=0)
    total = jnp.sum(stats_all[:, blocks : 2 * blocks] * jnp.exp(tops - top[None]), axis=0)
    log_a_all = stats_all[:, 2 * blocks]
    f_all = EPSILON * log_a_all - EPSILON * (top + jnp.log(total))
    f_new = lax.dynamic_index_in_dim(f_all, me, 0, False)

    f_col = (f_all[order] / EPSILON)[:, :, None]
    tile_top, tile_total = resident_call(
        col_kernel, my_ids, my_cnt, f_col, targets, [x_own, x_other], rows,
        jax.ShapeDtypeStruct((tiles_own, 1, width), jnp.float32), scale,
    )
    col = jnp.concatenate([tile_top.reshape(tiles_own, width), tile_total.reshape(tiles_own, width)])
    loop_size = lax.axis_size(LOOP)
    col_all = lax.all_to_all(
        jnp.broadcast_to(col[None], (loop_size,) + col.shape), LOOP, 0, 0, tiled=True
    )
    tops = col_all[:, :tiles_own]
    all_top = jnp.max(tops, axis=0)
    all_total = jnp.sum(col_all[:, tiles_own:] * jnp.exp(tops - all_top[None]), axis=0)
    g_new = EPSILON * log_b - EPSILON * (all_top + jnp.log(all_total))
    return (f_new, g_new)


PARTS = (("x_lo", 2), ("z", 4), ("core", 2), ("x_hi", 2), ("y", 4))
CHIPS = ("x_lo", "z")
CORE = "core"
SRC = ("x_lo", "z", "core")
LOOP = ("x_hi", "y")


def solution(mesh):
    parted = Mesh(
        mesh.devices.reshape(tuple(size for _, size in PARTS)), tuple(name for name, _ in PARTS)
    )
    rows_spec = SRC + LOOP
    return jax.shard_map(
        local_body,
        mesh=parted,
        in_specs=(
            P(rows_spec, None),
            P(rows_spec),
            P(SRC, None, None),
            P(SRC, None),
            P(SRC, None),
            P(rows_spec, None, None),
            P(rows_spec, None),
        ),
        out_specs=(P(rows_spec), P(SRC, None)),
        check_vma=False,
    )
```

```python
import math

import jax
import jax.numpy as jnp
from jax import lax
from jax.experimental import pallas as pl
from jax.experimental.pallas import tpu as pltpu
from jax.sharding import PartitionSpec as P

EPSILON = 0.1
VERY_LOW = -1e30
NT_DIMS = (((1,), (1,)), ((), ()))


def load_all(t_hbm, x_hbm, t_vmem, x_vmem, t_sem, x_sem, window):
    tiles, blocks = t_vmem.shape[0], x_vmem.shape[0]
    rows = x_vmem.shape[1]

    def x_copy(s):
        return pltpu.make_async_copy(x_hbm.at[s, pl.ds(0, rows)], x_vmem.at[s], x_sem.at[s])

    def t_copy(t):
        return pltpu.make_async_copy(t_hbm.at[t], t_vmem.at[t], t_sem.at[t])

    for t in range(tiles):
        t_copy(t).start()
    for s in range(min(window, blocks)):
        x_copy(s).start()
    for t in range(tiles):
        t_copy(t).wait()

    def arrive(s):
        x_copy(s).wait()

        @pl.when(s + window < blocks)
        def _():
            x_copy(jnp.minimum(s + window, blocks - 1)).start()

    return arrive


def row_kernel(ids_ref, cnt_ref, g_ref, t_hbm, x_hbm, top_ref, tot_ref, t_vmem, x_vmem, t_sem, x_sem, *, scale, slots, window):
    arrive = load_all(t_hbm, x_hbm, t_vmem, x_vmem, t_sem, x_sem, window)

    def step(s, carry):
        arrive(s)
        top_ref[s] = jnp.full(top_ref.shape[1:], VERY_LOW, jnp.float32)
        tot_ref[s] = jnp.zeros(tot_ref.shape[1:], jnp.float32)
        for c in range(slots):

            @pl.when(c < cnt_ref[s])
            def _():
                t = ids_ref[s * slots + c]
                kt = lax.dot_general(t_vmem[t], x_vmem[s], NT_DIMS, preferred_element_type=jnp.float32)
                logits = g_ref[t] + kt * scale
                old = top_ref[s]
                new = jnp.maximum(old, jnp.max(logits, axis=0, keepdims=True))
                tot_ref[s] = tot_ref[s] * jnp.exp(old - new) + jnp.sum(
                    jnp.exp(logits - new), axis=0, keepdims=True
                )
                top_ref[s] = new

        return carry

    lax.fori_loop(0, x_vmem.shape[0], step, 0)


def col_kernel(ids_ref, cnt_ref, f_ref, t_hbm, x_hbm, top_ref, tot_ref, t_vmem, x_vmem, t_sem, x_sem, *, scale, slots, window):
    arrive = load_all(t_hbm, x_hbm, t_vmem, x_vmem, t_sem, x_sem, window)
    top_ref[...] = jnp.full(top_ref.shape, VERY_LOW, jnp.float32)
    tot_ref[...] = jnp.zeros(tot_ref.shape, jnp.float32)

    def step(s, carry):
        arrive(s)
        for c in range(slots):

            @pl.when(c < cnt_ref[s])
            def _():
                t = ids_ref[s * slots + c]
                k = lax.dot_general(x_vmem[s], t_vmem[t], NT_DIMS, preferred_element_type=jnp.float32)
                logits = f_ref[s] + k * scale
                old = top_ref[t]
                new = jnp.maximum(old, jnp.max(logits, axis=0, keepdims=True))
                tot_ref[t] = tot_ref[t] * jnp.exp(old - new) + jnp.sum(
                    jnp.exp(logits - new), axis=0, keepdims=True
                )
                top_ref[t] = new

        return carry

    lax.fori_loop(0, x_vmem.shape[0], step, 0)


def resident_call(body, ids, cnt, side, targets, x_all, rows, out_shape, scale):
    tiles, width, depth = targets.shape
    blocks = x_all.shape[0]
    slots = ids.shape[1]
    smem = pl.BlockSpec(memory_space=pltpu.SMEM)
    vmem = pl.BlockSpec(memory_space=pltpu.VMEM)
    hbm = pl.BlockSpec(memory_space=pl.ANY)
    cost = pl.CostEstimate(
        flops=2 * blocks * slots * rows * width * depth,
        transcendentals=blocks * slots * rows * width,
        bytes_accessed=2 * (targets.size + blocks * rows * depth),
    )
    kernel = lambda *refs: body(*refs, scale=scale, slots=slots, window=16)
    return pl.pallas_call(
        kernel,
        out_shape=(out_shape, out_shape),
        in_specs=[smem, smem, vmem, hbm, hbm],
        out_specs=(vmem, vmem),
        scratch_shapes=[
            pltpu.VMEM((tiles, width, depth), targets.dtype),
            pltpu.VMEM((blocks, rows, depth), x_all.dtype),
            pltpu.SemaphoreType.DMA((tiles,)),
            pltpu.SemaphoreType.DMA((blocks,)),
        ],
        compiler_params=pltpu.CompilerParams(vmem_limit_bytes=56 * 1024 * 1024),
        cost_estimate=cost,
    )(ids.reshape(-1), cnt, side, targets, x_all)


def local(sources, log_a, targets, g_old, log_b, tile_ids, live_count):
    tiles_own, width, depth = targets.shape
    rows = sources.shape[0]
    slots_per = tile_ids.shape[2]
    groups = tile_ids.shape[1]
    me = lax.axis_index("src")
    scale = 1.0 / (math.sqrt(depth) * EPSILON)

    meta = jnp.concatenate([tile_ids[0].reshape(-1), live_count[0].reshape(-1)])
    meta_rows = jnp.zeros((16, depth), jnp.bfloat16).at[0, : meta.shape[0]].set(
        meta.astype(jnp.bfloat16)
    )
    packed = jnp.concatenate([sources, meta_rows], axis=0)
    x_all = lax.all_gather(packed, "src")
    meta_all = x_all[:, rows, : meta.shape[0]].astype(jnp.int32)
    blocks = x_all.shape[0]
    ids_all = meta_all[:, : groups * slots_per].reshape(blocks, groups, slots_per)
    cnt_all = meta_all[:, groups * slots_per :]
    my_ids = jnp.clip(lax.dynamic_index_in_dim(ids_all, me, 1, False) - me * tiles_own, 0, tiles_own - 1)
    my_cnt = lax.dynamic_index_in_dim(cnt_all, me, 1, False)

    g_col = (g_old.astype(jnp.float32) / EPSILON)[:, :, None]
    row_top, row_total = resident_call(
        row_kernel, my_ids, my_cnt, g_col, targets, x_all, rows,
        jax.ShapeDtypeStruct((blocks, 1, rows), jnp.float32), scale,
    )
    stats = jnp.concatenate(
        [row_top.reshape(blocks, rows), row_total.reshape(blocks, rows), log_a[None]], axis=0
    )
    stats_all = lax.all_to_all(
        jnp.broadcast_to(stats[None], (blocks,) + stats.shape), "src", 0, 0, tiled=True
    )
    tops = stats_all[:, :blocks]
    top = jnp.max(tops, axis=0)
    total = jnp.sum(stats_all[:, blocks : 2 * blocks] * jnp.exp(tops - top[None]), axis=0)
    log_a_all = stats_all[:, 2 * blocks]
    f_all = EPSILON * log_a_all - EPSILON * (top + jnp.log(total))
    f_new = lax.dynamic_index_in_dim(f_all, me, 0, False)

    f_col = (f_all / EPSILON)[:, :, None]
    tile_top, tile_total = resident_call(
        col_kernel, my_ids, my_cnt, f_col, targets, x_all, rows,
        jax.ShapeDtypeStruct((tiles_own, 1, width), jnp.float32), scale,
    )
    col = jnp.concatenate([tile_top.reshape(tiles_own, width), tile_total.reshape(tiles_own, width)])
    loop_size = lax.axis_size("loop")
    col_all = lax.all_to_all(
        jnp.broadcast_to(col[None], (loop_size,) + col.shape), "loop", 0, 0, tiled=True
    )
    tops = col_all[:, :tiles_own]
    all_top = jnp.max(tops, axis=0)
    all_total = jnp.sum(col_all[:, tiles_own:] * jnp.exp(tops - all_top[None]), axis=0)
    g_new = EPSILON * log_b - EPSILON * (all_top + jnp.log(all_total))
    return (f_new, g_new)


def solution(mesh):
    return jax.shard_map(
        local,
        mesh=mesh,
        in_specs=(
            P(("src", "loop"), None),
            P(("src", "loop")),
            P("src", None, None),
            P("src", None),
            P("src", None),
            P(("src", "loop"), None, None),
            P(("src", "loop"), None),
        ),
        out_specs=(P(("src", "loop")), P("src", None)),
        check_vma=False,
    )
```

```python
import math

import jax
import jax.numpy as jnp
from jax import lax
from jax.experimental import pallas as pl
from jax.experimental.pallas import tpu as pltpu
from jax.sharding import PartitionSpec as P

EPSILON = 0.1
VERY_LOW = -1e30
NT_DIMS = (((1,), (1,)), ((), ()))


def load_all(order_ref, t_hbm, x_hbm, t_vmem, x_vmem, t_sem, x_sem, flags, window):
    tiles, blocks = t_vmem.shape[0], x_vmem.shape[0]
    rows = x_vmem.shape[1]

    def x_copy(s):
        return pltpu.make_async_copy(x_hbm.at[s, pl.ds(0, rows)], x_vmem.at[s], x_sem.at[s])

    def t_copy(t):
        return pltpu.make_async_copy(t_hbm.at[t], t_vmem.at[t], t_sem.at[t])

    for t in range(tiles):
        flags[t] = 0
    issue = [("x", 0), ("t", 0), ("t", 1), ("x", 1), ("t", 2), ("x", 2), ("t", 3), ("x", 3)]
    issue = [item for item in issue if item[1] < (blocks if item[0] == "x" else tiles)]
    issue += [("x", s) for s in range(4, min(window, blocks))]
    issue += [("t", k) for k in range(4, tiles)]
    for kind, k in issue:
        if kind == "x":
            x_copy(k).start()
        else:
            t_copy(order_ref[k]).start()

    def arrive(s):
        x_copy(s).wait()

        @pl.when(s + window < blocks)
        def _():
            x_copy(jnp.minimum(s + window, blocks - 1)).start()

    def need(t):
        @pl.when(flags[t] == 0)
        def _():
            t_copy(t).wait()
            flags[t] = 1

    def finish():
        for t in range(tiles):
            need(t)

    return arrive, need, finish


def row_kernel(ids_ref, cnt_ref, order_ref, g_ref, t_hbm, x_hbm, top_ref, tot_ref, t_vmem, x_vmem, t_sem, x_sem, flags, *, scale, slots, window):
    arrive, need, finish = load_all(order_ref, t_hbm, x_hbm, t_vmem, x_vmem, t_sem, x_sem, flags, window)

    def step(s, carry):
        arrive(s)
        top_ref[s] = jnp.full(top_ref.shape[1:], VERY_LOW, jnp.float32)
        tot_ref[s] = jnp.zeros(tot_ref.shape[1:], jnp.float32)
        for c in range(slots):

            @pl.when(c < cnt_ref[s])
            def _():
                t = ids_ref[s * slots + c]
                need(t)
                kt = lax.dot_general(t_vmem[t], x_vmem[s], NT_DIMS, preferred_element_type=jnp.float32)
                logits = g_ref[t] + kt * scale
                old = top_ref[s]
                new = jnp.maximum(old, jnp.max(logits, axis=0, keepdims=True))
                tot_ref[s] = tot_ref[s] * jnp.exp(old - new) + jnp.sum(
                    jnp.exp(logits - new), axis=0, keepdims=True
                )
                top_ref[s] = new

        return carry

    lax.fori_loop(0, x_vmem.shape[0], step, 0)
    finish()


def col_kernel(ids_ref, cnt_ref, order_ref, f_ref, t_hbm, x_hbm, top_ref, tot_ref, t_vmem, x_vmem, t_sem, x_sem, flags, *, scale, slots, window):
    arrive, need, finish = load_all(order_ref, t_hbm, x_hbm, t_vmem, x_vmem, t_sem, x_sem, flags, window)
    top_ref[...] = jnp.full(top_ref.shape, VERY_LOW, jnp.float32)
    tot_ref[...] = jnp.zeros(tot_ref.shape, jnp.float32)

    def step(s, carry):
        arrive(s)
        for c in range(slots):

            @pl.when(c < cnt_ref[s])
            def _():
                t = ids_ref[s * slots + c]
                need(t)
                k = lax.dot_general(x_vmem[s], t_vmem[t], NT_DIMS, preferred_element_type=jnp.float32)
                logits = f_ref[s] + k * scale
                old = top_ref[t]
                new = jnp.maximum(old, jnp.max(logits, axis=0, keepdims=True))
                tot_ref[t] = tot_ref[t] * jnp.exp(old - new) + jnp.sum(
                    jnp.exp(logits - new), axis=0, keepdims=True
                )
                top_ref[t] = new

        return carry

    lax.fori_loop(0, x_vmem.shape[0], step, 0)
    finish()


def first_use_order(ids, cnt, tiles):
    blocks, slots = ids.shape
    live = jnp.arange(slots, dtype=jnp.int32)[None, :] < cnt[:, None]
    position = jnp.arange(blocks * slots, dtype=jnp.int32).reshape(blocks, slots)
    hit = (ids[:, :, None] == jnp.arange(tiles, dtype=jnp.int32)) & live[:, :, None]
    first = jnp.min(jnp.where(hit, position[:, :, None], blocks * slots), axis=(0, 1))
    return jnp.argsort(first).astype(jnp.int32)


def resident_call(body, ids, cnt, side, targets, x_all, rows, out_shape, scale):
    tiles, width, depth = targets.shape
    blocks = x_all.shape[0]
    slots = ids.shape[1]
    smem = pl.BlockSpec(memory_space=pltpu.SMEM)
    vmem = pl.BlockSpec(memory_space=pltpu.VMEM)
    hbm = pl.BlockSpec(memory_space=pl.ANY)
    cost = pl.CostEstimate(
        flops=2 * blocks * slots * rows * width * depth,
        transcendentals=blocks * slots * rows * width,
        bytes_accessed=2 * (targets.size + blocks * rows * depth),
    )
    kernel = lambda *refs: body(*refs, scale=scale, slots=slots, window=4)
    return pl.pallas_call(
        kernel,
        out_shape=(out_shape, out_shape),
        in_specs=[smem, smem, smem, vmem, hbm, hbm],
        out_specs=(vmem, vmem),
        scratch_shapes=[
            pltpu.VMEM((tiles, width, depth), targets.dtype),
            pltpu.VMEM((blocks, rows, depth), x_all.dtype),
            pltpu.SemaphoreType.DMA((tiles,)),
            pltpu.SemaphoreType.DMA((blocks,)),
            pltpu.SMEM((tiles,), jnp.int32),
        ],
        compiler_params=pltpu.CompilerParams(vmem_limit_bytes=56 * 1024 * 1024),
        cost_estimate=cost,
    )(ids.reshape(-1), cnt, first_use_order(ids, cnt, tiles), side, targets, x_all)


def local(sources, log_a, targets, g_old, log_b, tile_ids, live_count):
    tiles_own, width, depth = targets.shape
    rows = sources.shape[0]
    slots_per = tile_ids.shape[2]
    groups = tile_ids.shape[1]
    me = lax.axis_index("src")
    scale = 1.0 / (math.sqrt(depth) * EPSILON)

    meta = jnp.concatenate([tile_ids[0].reshape(-1), live_count[0].reshape(-1)])
    meta_rows = jnp.zeros((16, depth), jnp.bfloat16).at[0, : meta.shape[0]].set(
        meta.astype(jnp.bfloat16)
    )
    packed = jnp.concatenate([sources, meta_rows], axis=0)
    x_all = lax.all_gather(packed, "src")
    meta_all = x_all[:, rows, : meta.shape[0]].astype(jnp.int32)
    blocks = x_all.shape[0]
    ids_all = meta_all[:, : groups * slots_per].reshape(blocks, groups, slots_per)
    cnt_all = meta_all[:, groups * slots_per :]
    my_ids = jnp.clip(lax.dynamic_index_in_dim(ids_all, me, 1, False) - me * tiles_own, 0, tiles_own - 1)
    my_cnt = lax.dynamic_index_in_dim(cnt_all, me, 1, False)

    g_col = (g_old.astype(jnp.float32) / EPSILON)[:, :, None]
    row_top, row_total = resident_call(
        row_kernel, my_ids, my_cnt, g_col, targets, x_all, rows,
        jax.ShapeDtypeStruct((blocks, 1, rows), jnp.float32), scale,
    )
    stats = jnp.concatenate(
        [row_top.reshape(blocks, rows), row_total.reshape(blocks, rows), log_a[None]], axis=0
    )
    stats_all = lax.all_to_all(
        jnp.broadcast_to(stats[None], (blocks,) + stats.shape), "src", 0, 0, tiled=True
    )
    tops = stats_all[:, :blocks]
    top = jnp.max(tops, axis=0)
    total = jnp.sum(stats_all[:, blocks : 2 * blocks] * jnp.exp(tops - top[None]), axis=0)
    log_a_all = stats_all[:, 2 * blocks]
    f_all = EPSILON * log_a_all - EPSILON * (top + jnp.log(total))
    f_new = lax.dynamic_index_in_dim(f_all, me, 0, False)

    f_col = (f_all / EPSILON)[:, :, None]
    tile_top, tile_total = resident_call(
        col_kernel, my_ids, my_cnt, f_col, targets, x_all, rows,
        jax.ShapeDtypeStruct((tiles_own, 1, width), jnp.float32), scale,
    )
    col = jnp.concatenate([tile_top.reshape(tiles_own, width), tile_total.reshape(tiles_own, width)])
    loop_size = lax.axis_size("loop")
    col_all = lax.all_to_all(
        jnp.broadcast_to(col[None], (loop_size,) + col.shape), "loop", 0, 0, tiled=True
    )
    tops = col_all[:, :tiles_own]
    all_top = jnp.max(tops, axis=0)
    all_total = jnp.sum(col_all[:, tiles_own:] * jnp.exp(tops - all_top[None]), axis=0)
    g_new = EPSILON * log_b - EPSILON * (all_top + jnp.log(all_total))
    return (f_new, g_new)


def solution(mesh):
    return jax.shard_map(
        local,
        mesh=mesh,
        in_specs=(
            P(("src", "loop"), None),
            P(("src", "loop")),
            P("src", None, None),
            P("src", None),
            P("src", None),
            P(("src", "loop"), None, None),
            P(("src", "loop"), None),
        ),
        out_specs=(P(("src", "loop")), P("src", None)),
        check_vma=False,
    )
```

```python
import math

import jax
import jax.numpy as jnp
from jax import lax
from jax.experimental import pallas as pl
from jax.experimental.pallas import tpu as pltpu
from jax.sharding import Mesh, PartitionSpec as P

EPSILON = 0.1
VERY_LOW = -1e30
NT_DIMS = (((1,), (1,)), ((), ()))


def load_all(order_ref, t_hbm, x_hbm, t_vmem, x_vmem, t_sem, x_sem, flags, window):
    tiles, blocks = t_vmem.shape[0], x_vmem.shape[0]
    rows = x_vmem.shape[1]

    def x_copy(s):
        return pltpu.make_async_copy(x_hbm.at[s, pl.ds(0, rows)], x_vmem.at[s], x_sem.at[s])

    def t_copy(t):
        return pltpu.make_async_copy(t_hbm.at[t], t_vmem.at[t], t_sem.at[t])

    for t in range(tiles):
        flags[t] = 0
    issue = [("x", 0), ("t", 0), ("t", 1), ("x", 1), ("t", 2), ("x", 2), ("t", 3), ("x", 3)]
    issue = [item for item in issue if item[1] < (blocks if item[0] == "x" else tiles)]
    issue += [("x", s) for s in range(4, min(window, blocks))]
    issue += [("t", k) for k in range(4, tiles)]
    for kind, k in issue:
        if kind == "x":
            x_copy(k).start()
        else:
            t_copy(order_ref[k]).start()

    def arrive(s):
        x_copy(s).wait()

        @pl.when(s + window < blocks)
        def _():
            x_copy(jnp.minimum(s + window, blocks - 1)).start()

    def need(t):
        @pl.when(flags[t] == 0)
        def _():
            t_copy(t).wait()
            flags[t] = 1

    def finish():
        for t in range(tiles):
            need(t)

    return arrive, need, finish


def row_kernel(ids_ref, cnt_ref, order_ref, g_ref, t_hbm, x_hbm, top_ref, tot_ref, t_vmem, x_vmem, t_sem, x_sem, flags, *, scale, slots, window):
    arrive, need, finish = load_all(order_ref, t_hbm, x_hbm, t_vmem, x_vmem, t_sem, x_sem, flags, window)

    def step(s, carry):
        arrive(s)
        top_ref[s] = jnp.full(top_ref.shape[1:], VERY_LOW, jnp.float32)
        tot_ref[s] = jnp.zeros(tot_ref.shape[1:], jnp.float32)
        for c in range(slots):

            @pl.when(c < cnt_ref[s])
            def _():
                t = ids_ref[s * slots + c]
                need(t)
                kt = lax.dot_general(t_vmem[t], x_vmem[s], NT_DIMS, preferred_element_type=jnp.float32)
                logits = g_ref[t] + kt * scale
                old = top_ref[s]
                new = jnp.maximum(old, jnp.max(logits, axis=0, keepdims=True))
                tot_ref[s] = tot_ref[s] * jnp.exp(old - new) + jnp.sum(
                    jnp.exp(logits - new), axis=0, keepdims=True
                )
                top_ref[s] = new

        return carry

    lax.fori_loop(0, x_vmem.shape[0], step, 0)
    finish()


def col_kernel(ids_ref, cnt_ref, order_ref, f_ref, t_hbm, x_hbm, top_ref, tot_ref, t_vmem, x_vmem, t_sem, x_sem, flags, *, scale, slots, window):
    arrive, need, finish = load_all(order_ref, t_hbm, x_hbm, t_vmem, x_vmem, t_sem, x_sem, flags, window)
    top_ref[...] = jnp.full(top_ref.shape, VERY_LOW, jnp.float32)
    tot_ref[...] = jnp.zeros(tot_ref.shape, jnp.float32)

    def step(s, carry):
        arrive(s)
        for c in range(slots):

            @pl.when(c < cnt_ref[s])
            def _():
                t = ids_ref[s * slots + c]
                need(t)
                k = lax.dot_general(x_vmem[s], t_vmem[t], NT_DIMS, preferred_element_type=jnp.float32)
                logits = f_ref[s] + k * scale
                old = top_ref[t]
                new = jnp.maximum(old, jnp.max(logits, axis=0, keepdims=True))
                tot_ref[t] = tot_ref[t] * jnp.exp(old - new) + jnp.sum(
                    jnp.exp(logits - new), axis=0, keepdims=True
                )
                top_ref[t] = new

        return carry

    lax.fori_loop(0, x_vmem.shape[0], step, 0)
    finish()


def first_use_order(ids, cnt, tiles):
    blocks, slots = ids.shape
    live = jnp.arange(slots, dtype=jnp.int32)[None, :] < cnt[:, None]
    position = jnp.arange(blocks * slots, dtype=jnp.int32).reshape(blocks, slots)
    hit = (ids[:, :, None] == jnp.arange(tiles, dtype=jnp.int32)) & live[:, :, None]
    first = jnp.min(jnp.where(hit, position[:, :, None], blocks * slots), axis=(0, 1))
    return jnp.argsort(first).astype(jnp.int32)


def resident_call(body, ids, cnt, side, targets, x_all, rows, out_shape, scale):
    tiles, width, depth = targets.shape
    blocks = x_all.shape[0]
    slots = ids.shape[1]
    smem = pl.BlockSpec(memory_space=pltpu.SMEM)
    vmem = pl.BlockSpec(memory_space=pltpu.VMEM)
    hbm = pl.BlockSpec(memory_space=pl.ANY)
    cost = pl.CostEstimate(
        flops=2 * blocks * slots * rows * width * depth,
        transcendentals=blocks * slots * rows * width,
        bytes_accessed=2 * (targets.size + blocks * rows * depth),
    )
    kernel = lambda *refs: body(*refs, scale=scale, slots=slots, window=4)
    return pl.pallas_call(
        kernel,
        out_shape=(out_shape, out_shape),
        in_specs=[smem, smem, smem, vmem, hbm, hbm],
        out_specs=(vmem, vmem),
        scratch_shapes=[
            pltpu.VMEM((tiles, width, depth), targets.dtype),
            pltpu.VMEM((blocks, rows, depth), x_all.dtype),
            pltpu.SemaphoreType.DMA((tiles,)),
            pltpu.SemaphoreType.DMA((blocks,)),
            pltpu.SMEM((tiles,), jnp.int32),
        ],
        compiler_params=pltpu.CompilerParams(vmem_limit_bytes=56 * 1024 * 1024),
        cost_estimate=cost,
    )(ids.reshape(-1), cnt, first_use_order(ids, cnt, tiles), side, targets, x_all)


def local(sources, log_a, targets, g_old, log_b, tile_ids, live_count):
    tiles_own, width, depth = targets.shape
    rows = sources.shape[0]
    slots_per = tile_ids.shape[2]
    groups = tile_ids.shape[1]
    me = lax.axis_index(SRC)
    scale = 1.0 / (math.sqrt(depth) * EPSILON)

    meta = jnp.concatenate([tile_ids[0].reshape(-1), live_count[0].reshape(-1)])
    meta_rows = jnp.zeros((16, depth), jnp.bfloat16).at[0, : meta.shape[0]].set(
        meta.astype(jnp.bfloat16)
    )
    packed = jnp.concatenate([sources, meta_rows], axis=0)
    x_pair = lax.all_gather(packed, CROSS)
    x_all = lax.all_gather(x_pair, ALONG)
    cross, along = x_all.shape[1], x_all.shape[0]
    blocks = cross * along
    x_all = x_all.reshape((blocks,) + packed.shape)
    position = jnp.arange(blocks, dtype=jnp.int32)
    order = (position % cross) * along + position // cross
    inverse = jnp.argsort(order)
    meta_all = x_all[:, rows, : meta.shape[0]].astype(jnp.int32)
    ids_all = meta_all[:, : groups * slots_per].reshape(blocks, groups, slots_per)
    cnt_all = meta_all[:, groups * slots_per :]
    my_ids = jnp.clip(lax.dynamic_index_in_dim(ids_all, me, 1, False) - me * tiles_own, 0, tiles_own - 1)
    my_cnt = lax.dynamic_index_in_dim(cnt_all, me, 1, False)

    g_col = (g_old.astype(jnp.float32) / EPSILON)[:, :, None]
    row_top, row_total = resident_call(
        row_kernel, my_ids, my_cnt, g_col, targets, x_all, rows,
        jax.ShapeDtypeStruct((blocks, 1, rows), jnp.float32), scale,
    )
    stats = jnp.concatenate(
        [row_top.reshape(blocks, rows)[inverse], row_total.reshape(blocks, rows)[inverse], log_a[None]],
        axis=0,
    )
    stats_all = lax.all_to_all(
        jnp.broadcast_to(stats[None], (blocks,) + stats.shape), SRC, 0, 0, tiled=True
    )
    tops = stats_all[:, :blocks]
    top = jnp.max(tops, axis=0)
    total = jnp.sum(stats_all[:, blocks : 2 * blocks] * jnp.exp(tops - top[None]), axis=0)
    log_a_all = stats_all[:, 2 * blocks]
    f_all = EPSILON * log_a_all - EPSILON * (top + jnp.log(total))
    f_new = lax.dynamic_index_in_dim(f_all, me, 0, False)

    f_col = (f_all[order] / EPSILON)[:, :, None]
    tile_top, tile_total = resident_call(
        col_kernel, my_ids, my_cnt, f_col, targets, x_all, rows,
        jax.ShapeDtypeStruct((tiles_own, 1, width), jnp.float32), scale,
    )
    col = jnp.concatenate([tile_top.reshape(tiles_own, width), tile_total.reshape(tiles_own, width)])
    loop_size = lax.axis_size(LOOP)
    col_all = lax.all_to_all(
        jnp.broadcast_to(col[None], (loop_size,) + col.shape), LOOP, 0, 0, tiled=True
    )
    tops = col_all[:, :tiles_own]
    all_top = jnp.max(tops, axis=0)
    all_total = jnp.sum(col_all[:, tiles_own:] * jnp.exp(tops - all_top[None]), axis=0)
    g_new = EPSILON * log_b - EPSILON * (all_top + jnp.log(all_total))
    return (f_new, g_new)


PARTS = (("x_lo", 2), ("z", 4), ("core", 2), ("x_hi", 2), ("y", 4))
CROSS = "x_lo"
ALONG = ("z", "core")
SRC = ("x_lo", "z", "core")
LOOP = ("x_hi", "y")


def solution(mesh):
    parted = Mesh(
        mesh.devices.reshape(tuple(size for _, size in PARTS)), tuple(name for name, _ in PARTS)
    )
    rows_spec = SRC + LOOP
    return jax.shard_map(
        local,
        mesh=parted,
        in_specs=(
            P(rows_spec, None),
            P(rows_spec),
            P(SRC, None, None),
            P(SRC, None),
            P(SRC, None),
            P(rows_spec, None, None),
            P(rows_spec, None),
        ),
        out_specs=(P(rows_spec), P(SRC, None)),
        check_vma=False,
    )
```

```python
import math

import jax
import jax.numpy as jnp
from jax import lax
from jax.experimental import pallas as pl
from jax.experimental.pallas import tpu as pltpu
from jax.sharding import PartitionSpec as P

EPSILON = 0.1
VERY_LOW = -1e30
NT_DIMS = (((1,), (1,)), ((), ()))


def load_all(order_ref, t_hbm, x_hbm, t_vmem, x_vmem, t_sem, x_sem, flags, window):
    tiles, blocks = t_vmem.shape[0], x_vmem.shape[0]
    rows = x_vmem.shape[1]

    def x_copy(s):
        return pltpu.make_async_copy(x_hbm.at[s, pl.ds(0, rows)], x_vmem.at[s], x_sem.at[s])

    def t_copy(t):
        return pltpu.make_async_copy(t_hbm.at[t], t_vmem.at[t], t_sem.at[t])

    for t in range(tiles):
        flags[t] = 0
    issue = [("x", 0), ("t", 0), ("t", 1), ("x", 1), ("t", 2), ("x", 2), ("t", 3), ("x", 3)]
    issue = [item for item in issue if item[1] < (blocks if item[0] == "x" else tiles)]
    issue += [("x", s) for s in range(4, min(window, blocks))]
    issue += [("t", k) for k in range(4, tiles)]
    for kind, k in issue:
        if kind == "x":
            x_copy(k).start()
        else:
            t_copy(order_ref[k]).start()

    def arrive(s):
        x_copy(s).wait()

        @pl.when(s + window < blocks)
        def _():
            x_copy(jnp.minimum(s + window, blocks - 1)).start()

    def need(t):
        @pl.when(flags[t] == 0)
        def _():
            t_copy(t).wait()
            flags[t] = 1

    def finish():
        for t in range(tiles):
            need(t)

    return arrive, need, finish


def row_kernel(ids_ref, cnt_ref, order_ref, g_ref, t_hbm, x_hbm, top_ref, tot_ref, t_vmem, x_vmem, t_sem, x_sem, flags, *, scale, slots, window):
    arrive, need, finish = load_all(order_ref, t_hbm, x_hbm, t_vmem, x_vmem, t_sem, x_sem, flags, window)

    def step(s, carry):
        arrive(s)
        top_ref[s] = jnp.full(top_ref.shape[1:], VERY_LOW, jnp.float32)
        tot_ref[s] = jnp.zeros(tot_ref.shape[1:], jnp.float32)
        for c in range(slots):

            @pl.when(c < cnt_ref[s])
            def _():
                t = ids_ref[s * slots + c]
                need(t)
                kt = lax.dot_general(t_vmem[t], x_vmem[s], NT_DIMS, preferred_element_type=jnp.float32)
                logits = g_ref[t] + kt * scale
                old = top_ref[s]
                new = jnp.maximum(old, jnp.max(logits, axis=0, keepdims=True))
                tot_ref[s] = tot_ref[s] * jnp.exp(old - new) + jnp.sum(
                    jnp.exp(logits - new), axis=0, keepdims=True
                )
                top_ref[s] = new

        return carry

    lax.fori_loop(0, x_vmem.shape[0], step, 0)
    finish()


def col_kernel(ids_ref, cnt_ref, order_ref, f_ref, t_hbm, x_hbm, top_ref, tot_ref, t_vmem, x_vmem, t_sem, x_sem, flags, *, scale, slots, window):
    arrive, need, finish = load_all(order_ref, t_hbm, x_hbm, t_vmem, x_vmem, t_sem, x_sem, flags, window)
    top_ref[...] = jnp.full(top_ref.shape, VERY_LOW, jnp.float32)
    tot_ref[...] = jnp.zeros(tot_ref.shape, jnp.float32)

    def step(s, carry):
        arrive(s)
        for c in range(slots):

            @pl.when(c < cnt_ref[s])
            def _():
                t = ids_ref[s * slots + c]
                need(t)
                k = lax.dot_general(x_vmem[s], t_vmem[t], NT_DIMS, preferred_element_type=jnp.float32)
                logits = f_ref[s] + k * scale
                old = top_ref[t]
                new = jnp.maximum(old, jnp.max(logits, axis=0, keepdims=True))
                tot_ref[t] = tot_ref[t] * jnp.exp(old - new) + jnp.sum(
                    jnp.exp(logits - new), axis=0, keepdims=True
                )
                top_ref[t] = new

        return carry

    lax.fori_loop(0, x_vmem.shape[0], step, 0)
    finish()


def first_use_order(ids, cnt, tiles):
    blocks, slots = ids.shape
    live = jnp.arange(slots, dtype=jnp.int32)[None, :] < cnt[:, None]
    position = jnp.arange(blocks * slots, dtype=jnp.int32).reshape(blocks, slots)
    hit = (ids[:, :, None] == jnp.arange(tiles, dtype=jnp.int32)) & live[:, :, None]
    first = jnp.min(jnp.where(hit, position[:, :, None], blocks * slots), axis=(0, 1))
    return jnp.argsort(first).astype(jnp.int32)


def resident_call(body, ids, cnt, side, targets, x_all, rows, out_shape, scale):
    tiles, width, depth = targets.shape
    blocks = x_all.shape[0]
    slots = ids.shape[1]
    smem = pl.BlockSpec(memory_space=pltpu.SMEM)
    vmem = pl.BlockSpec(memory_space=pltpu.VMEM)
    hbm = pl.BlockSpec(memory_space=pl.ANY)
    cost = pl.CostEstimate(
        flops=2 * blocks * slots * rows * width * depth,
        transcendentals=blocks * slots * rows * width,
        bytes_accessed=2 * (targets.size + blocks * rows * depth),
    )
    kernel = lambda *refs: body(*refs, scale=scale, slots=slots, window=4)
    return pl.pallas_call(
        kernel,
        out_shape=(out_shape, out_shape),
        in_specs=[smem, smem, smem, vmem, hbm, hbm],
        out_specs=(vmem, vmem),
        scratch_shapes=[
            pltpu.VMEM((tiles, width, depth), targets.dtype),
            pltpu.VMEM((blocks, rows, depth), x_all.dtype),
            pltpu.SemaphoreType.DMA((tiles,)),
            pltpu.SemaphoreType.DMA((blocks,)),
            pltpu.SMEM((tiles,), jnp.int32),
        ],
        compiler_params=pltpu.CompilerParams(vmem_limit_bytes=56 * 1024 * 1024),
        cost_estimate=cost,
    )(ids.reshape(-1), cnt, first_use_order(ids, cnt, tiles), side, targets, x_all)


def local(sources, log_a, targets, g_old, log_b, tile_ids, live_count):
    tiles_own, width, depth = targets.shape
    rows = sources.shape[0]
    slots_per = tile_ids.shape[2]
    groups = tile_ids.shape[1]
    me = lax.axis_index("src")
    scale = 1.0 / (math.sqrt(depth) * EPSILON)

    meta = jnp.concatenate([tile_ids[0].reshape(-1), live_count[0].reshape(-1)])
    meta_rows = jnp.zeros((16, depth), jnp.bfloat16).at[0, : meta.shape[0]].set(
        meta.astype(jnp.bfloat16)
    )
    packed = jnp.concatenate([sources, meta_rows], axis=0)
    x_all = lax.all_gather(packed, "src")
    meta_all = x_all[:, rows, : meta.shape[0]].astype(jnp.int32)
    blocks = x_all.shape[0]
    ids_all = meta_all[:, : groups * slots_per].reshape(blocks, groups, slots_per)
    cnt_all = meta_all[:, groups * slots_per :]
    my_ids = jnp.clip(lax.dynamic_index_in_dim(ids_all, me, 1, False) - me * tiles_own, 0, tiles_own - 1)
    my_cnt = lax.dynamic_index_in_dim(cnt_all, me, 1, False)

    g_col = (g_old.astype(jnp.float32) / EPSILON)[:, :, None]
    row_top, row_total = resident_call(
        row_kernel, my_ids, my_cnt, g_col, targets, x_all, rows,
        jax.ShapeDtypeStruct((blocks, 1, rows), jnp.float32), scale,
    )
    sent = jnp.stack([row_top.reshape(blocks, rows), row_total.reshape(blocks, rows)], axis=1)
    got = lax.all_to_all(sent, "src", 0, 0, tiled=True)
    top = jnp.max(got[:, 0], axis=0)
    total = jnp.sum(got[:, 1] * jnp.exp(got[:, 0] - top[None]), axis=0)
    f_new = EPSILON * log_a - EPSILON * (top + jnp.log(total))
    f_all = lax.all_to_all(
        jnp.broadcast_to(f_new[None], (blocks,) + f_new.shape), "src", 0, 0, tiled=True
    )

    f_col = (f_all / EPSILON)[:, :, None]
    tile_top, tile_total = resident_call(
        col_kernel, my_ids, my_cnt, f_col, targets, x_all, rows,
        jax.ShapeDtypeStruct((tiles_own, 1, width), jnp.float32), scale,
    )
    col = jnp.concatenate([tile_top.reshape(tiles_own, width), tile_total.reshape(tiles_own, width)])
    loop_size = lax.axis_size("loop")
    col_all = lax.all_to_all(
        jnp.broadcast_to(col[None], (loop_size,) + col.shape), "loop", 0, 0, tiled=True
    )
    tops = col_all[:, :tiles_own]
    all_top = jnp.max(tops, axis=0)
    all_total = jnp.sum(col_all[:, tiles_own:] * jnp.exp(tops - all_top[None]), axis=0)
    g_new = EPSILON * log_b - EPSILON * (all_top + jnp.log(all_total))
    return (f_new, g_new)


def solution(mesh):
    return jax.shard_map(
        local,
        mesh=mesh,
        in_specs=(
            P(("src", "loop"), None),
            P(("src", "loop")),
            P("src", None, None),
            P("src", None),
            P("src", None),
            P(("src", "loop"), None, None),
            P(("src", "loop"), None),
        ),
        out_specs=(P(("src", "loop")), P("src", None)),
        check_vma=False,
    )
```

```python
import math

import jax
import jax.numpy as jnp
from jax import lax
from jax.experimental import pallas as pl
from jax.experimental.pallas import tpu as pltpu
from jax.sharding import PartitionSpec as P

EPSILON = 0.1
VERY_LOW = -1e30
LOG2E = 1.0 / math.log(2.0)
LN2 = math.log(2.0)
NT_DIMS = (((1,), (1,)), ((), ()))


def load_all(order_ref, t_hbm, x_hbm, t_vmem, x_vmem, t_sem, x_sem, flags, window):
    tiles, blocks = t_vmem.shape[0], x_vmem.shape[0]
    rows = x_vmem.shape[1]

    def x_copy(s):
        return pltpu.make_async_copy(x_hbm.at[s, pl.ds(0, rows)], x_vmem.at[s], x_sem.at[s])

    def t_copy(t):
        return pltpu.make_async_copy(t_hbm.at[t], t_vmem.at[t], t_sem.at[t])

    for t in range(tiles):
        flags[t] = 0
    issue = [("x", 0), ("t", 0), ("t", 1), ("x", 1), ("t", 2), ("x", 2), ("t", 3), ("x", 3)]
    issue = [item for item in issue if item[1] < (blocks if item[0] == "x" else tiles)]
    issue += [("x", s) for s in range(4, min(window, blocks))]
    issue += [("t", k) for k in range(4, tiles)]
    for kind, k in issue:
        if kind == "x":
            x_copy(k).start()
        else:
            t_copy(order_ref[k]).start()

    def arrive(s):
        x_copy(s).wait()

        @pl.when(s + window < blocks)
        def _():
            x_copy(jnp.minimum(s + window, blocks - 1)).start()

    def need(t):
        @pl.when(flags[t] == 0)
        def _():
            t_copy(t).wait()
            flags[t] = 1

    def finish():
        for t in range(tiles):
            need(t)

    return arrive, need, finish


def row_kernel(ids_ref, cnt_ref, order_ref, g_ref, t_hbm, x_hbm, top_ref, tot_ref, t_vmem, x_vmem, t_sem, x_sem, flags, *, scale, slots, window):
    arrive, need, finish = load_all(order_ref, t_hbm, x_hbm, t_vmem, x_vmem, t_sem, x_sem, flags, window)

    def step(s, carry):
        arrive(s)
        top_ref[s] = jnp.full(top_ref.shape[1:], VERY_LOW, jnp.float32)
        tot_ref[s] = jnp.zeros(tot_ref.shape[1:], jnp.float32)
        for c in range(slots):

            @pl.when(c < cnt_ref[s])
            def _():
                t = ids_ref[s * slots + c]
                need(t)
                kt = lax.dot_general(t_vmem[t], x_vmem[s], NT_DIMS, preferred_element_type=jnp.float32)
                logits = g_ref[t] + kt * scale
                old = top_ref[s]
                new = jnp.maximum(old, jnp.max(logits, axis=0, keepdims=True))
                tot_ref[s] = tot_ref[s] * jnp.exp2(old - new) + jnp.sum(
                    jnp.exp2(logits - new), axis=0, keepdims=True
                )
                top_ref[s] = new

        return carry

    lax.fori_loop(0, x_vmem.shape[0], step, 0)
    finish()


def col_kernel(ids_ref, cnt_ref, order_ref, f_ref, t_hbm, x_hbm, top_ref, tot_ref, t_vmem, x_vmem, t_sem, x_sem, flags, *, scale, slots, window):
    arrive, need, finish = load_all(order_ref, t_hbm, x_hbm, t_vmem, x_vmem, t_sem, x_sem, flags, window)
    top_ref[...] = jnp.full(top_ref.shape, VERY_LOW, jnp.float32)
    tot_ref[...] = jnp.zeros(tot_ref.shape, jnp.float32)

    def step(s, carry):
        arrive(s)
        for c in range(slots):

            @pl.when(c < cnt_ref[s])
            def _():
                t = ids_ref[s * slots + c]
                need(t)
                k = lax.dot_general(x_vmem[s], t_vmem[t], NT_DIMS, preferred_element_type=jnp.float32)
                logits = f_ref[s] + k * scale
                old = top_ref[t]
                new = jnp.maximum(old, jnp.max(logits, axis=0, keepdims=True))
                tot_ref[t] = tot_ref[t] * jnp.exp2(old - new) + jnp.sum(
                    jnp.exp2(logits - new), axis=0, keepdims=True
                )
                top_ref[t] = new

        return carry

    lax.fori_loop(0, x_vmem.shape[0], step, 0)
    finish()


def first_use_order(ids, cnt, tiles):
    blocks, slots = ids.shape
    live = jnp.arange(slots, dtype=jnp.int32)[None, :] < cnt[:, None]
    position = jnp.arange(blocks * slots, dtype=jnp.int32).reshape(blocks, slots)
    hit = (ids[:, :, None] == jnp.arange(tiles, dtype=jnp.int32)) & live[:, :, None]
    first = jnp.min(jnp.where(hit, position[:, :, None], blocks * slots), axis=(0, 1))
    return jnp.argsort(first).astype(jnp.int32)


def resident_call(body, ids, cnt, side, targets, x_all, rows, out_shape, scale):
    tiles, width, depth = targets.shape
    blocks = x_all.shape[0]
    slots = ids.shape[1]
    smem = pl.BlockSpec(memory_space=pltpu.SMEM)
    vmem = pl.BlockSpec(memory_space=pltpu.VMEM)
    hbm = pl.BlockSpec(memory_space=pl.ANY)
    cost = pl.CostEstimate(
        flops=2 * blocks * slots * rows * width * depth,
        transcendentals=blocks * slots * rows * width,
        bytes_accessed=2 * (targets.size + blocks * rows * depth),
    )
    kernel = lambda *refs: body(*refs, scale=scale, slots=slots, window=4)
    return pl.pallas_call(
        kernel,
        out_shape=(out_shape, out_shape),
        in_specs=[smem, smem, smem, vmem, hbm, hbm],
        out_specs=(vmem, vmem),
        scratch_shapes=[
            pltpu.VMEM((tiles, width, depth), targets.dtype),
            pltpu.VMEM((blocks, rows, depth), x_all.dtype),
            pltpu.SemaphoreType.DMA((tiles,)),
            pltpu.SemaphoreType.DMA((blocks,)),
            pltpu.SMEM((tiles,), jnp.int32),
        ],
        compiler_params=pltpu.CompilerParams(vmem_limit_bytes=56 * 1024 * 1024),
        cost_estimate=cost,
    )(ids.reshape(-1), cnt, first_use_order(ids, cnt, tiles), side, targets, x_all)


def local(sources, log_a, targets, g_old, log_b, tile_ids, live_count):
    tiles_own, width, depth = targets.shape
    rows = sources.shape[0]
    slots_per = tile_ids.shape[2]
    groups = tile_ids.shape[1]
    me = lax.axis_index("src")
    scale = LOG2E / (math.sqrt(depth) * EPSILON)

    meta = jnp.concatenate([tile_ids[0].reshape(-1), live_count[0].reshape(-1)])
    meta_rows = jnp.zeros((16, depth), jnp.bfloat16).at[0, : meta.shape[0]].set(
        meta.astype(jnp.bfloat16)
    )
    packed = jnp.concatenate([sources, meta_rows], axis=0)
    x_all = lax.all_gather(packed, "src")
    meta_all = x_all[:, rows, : meta.shape[0]].astype(jnp.int32)
    blocks = x_all.shape[0]
    ids_all = meta_all[:, : groups * slots_per].reshape(blocks, groups, slots_per)
    cnt_all = meta_all[:, groups * slots_per :]
    my_ids = jnp.clip(lax.dynamic_index_in_dim(ids_all, me, 1, False) - me * tiles_own, 0, tiles_own - 1)
    my_cnt = lax.dynamic_index_in_dim(cnt_all, me, 1, False)

    g_col = (g_old.astype(jnp.float32) * (LOG2E / EPSILON))[:, :, None]
    row_top, row_total = resident_call(
        row_kernel, my_ids, my_cnt, g_col, targets, x_all, rows,
        jax.ShapeDtypeStruct((blocks, 1, rows), jnp.float32), scale,
    )
    sent = jnp.stack([row_top.reshape(blocks, rows), row_total.reshape(blocks, rows)], axis=1)
    got = lax.all_to_all(sent, "src", 0, 0, tiled=True)
    top = jnp.max(got[:, 0], axis=0)
    total = jnp.sum(got[:, 1] * jnp.exp2(got[:, 0] - top[None]), axis=0)
    f_new = EPSILON * log_a - EPSILON * (top * LN2 + jnp.log(total))
    f_all = lax.all_to_all(
        jnp.broadcast_to(f_new[None], (blocks,) + f_new.shape), "src", 0, 0, tiled=True
    )

    f_col = (f_all * (LOG2E / EPSILON))[:, :, None]
    tile_top, tile_total = resident_call(
        col_kernel, my_ids, my_cnt, f_col, targets, x_all, rows,
        jax.ShapeDtypeStruct((tiles_own, 1, width), jnp.float32), scale,
    )
    col = jnp.concatenate([tile_top.reshape(tiles_own, width), tile_total.reshape(tiles_own, width)])
    loop_size = lax.axis_size("loop")
    col_all = lax.all_to_all(
        jnp.broadcast_to(col[None], (loop_size,) + col.shape), "loop", 0, 0, tiled=True
    )
    tops = col_all[:, :tiles_own]
    all_top = jnp.max(tops, axis=0)
    all_total = jnp.sum(col_all[:, tiles_own:] * jnp.exp2(tops - all_top[None]), axis=0)
    g_new = EPSILON * log_b - EPSILON * (all_top * LN2 + jnp.log(all_total))
    return (f_new, g_new)


def solution(mesh):
    return jax.shard_map(
        local,
        mesh=mesh,
        in_specs=(
            P(("src", "loop"), None),
            P(("src", "loop")),
            P("src", None, None),
            P("src", None),
            P("src", None),
            P(("src", "loop"), None, None),
            P(("src", "loop"), None),
        ),
        out_specs=(P(("src", "loop")), P("src", None)),
        check_vma=False,
    )
```

```python
import math

import jax
import jax.numpy as jnp
from jax import lax
from jax.experimental import pallas as pl
from jax.experimental.pallas import tpu as pltpu
from jax.sharding import PartitionSpec as P

EPSILON = 0.1
VERY_LOW = -1e30
NT_DIMS = (((1,), (1,)), ((), ()))


def load_all(order_ref, t_hbm, x_hbm, t_vmem, x_vmem, t_sem, x_sem, flags, window):
    tiles, blocks = t_vmem.shape[0], x_vmem.shape[0]
    rows = x_vmem.shape[1]

    def x_copy(s):
        return pltpu.make_async_copy(x_hbm.at[s, pl.ds(0, rows)], x_vmem.at[s], x_sem.at[s])

    def t_copy(t):
        return pltpu.make_async_copy(t_hbm.at[t], t_vmem.at[t], t_sem.at[t])

    for t in range(tiles):
        flags[t] = 0
    issue = [("x", 0), ("t", 0), ("t", 1), ("x", 1), ("t", 2), ("x", 2), ("t", 3), ("x", 3)]
    issue = [item for item in issue if item[1] < (blocks if item[0] == "x" else tiles)]
    issue += [("x", s) for s in range(4, min(window, blocks))]
    issue += [("t", k) for k in range(4, tiles)]
    for kind, k in issue:
        if kind == "x":
            x_copy(k).start()
        else:
            t_copy(order_ref[k]).start()

    def arrive(s):
        x_copy(s).wait()

        @pl.when(s + window < blocks)
        def _():
            x_copy(jnp.minimum(s + window, blocks - 1)).start()

    def need(t):
        @pl.when(flags[t] == 0)
        def _():
            t_copy(t).wait()
            flags[t] = 1

    def finish():
        for t in range(tiles):
            need(t)

    return arrive, need, finish


def row_kernel(ids_ref, cnt_ref, order_ref, g_ref, t_hbm, x_hbm, top_ref, tot_ref, t_vmem, x_vmem, t_sem, x_sem, flags, *, scale, slots, window):
    arrive, need, finish = load_all(order_ref, t_hbm, x_hbm, t_vmem, x_vmem, t_sem, x_sem, flags, window)

    def step(s, carry):
        arrive(s)
        top_ref[s] = jnp.full(top_ref.shape[1:], VERY_LOW, jnp.float32)
        tot_ref[s] = jnp.zeros(tot_ref.shape[1:], jnp.float32)
        for c in range(slots):

            @pl.when(c < cnt_ref[s])
            def _():
                t = ids_ref[s * slots + c]
                need(t)
                kt = lax.dot_general(t_vmem[t], x_vmem[s], NT_DIMS, preferred_element_type=jnp.float32)
                logits = g_ref[t] + kt * scale
                old = top_ref[s]
                new = jnp.maximum(old, jnp.max(logits, axis=0, keepdims=True))
                tot_ref[s] = tot_ref[s] * jnp.exp(old - new) + jnp.sum(
                    jnp.exp(logits - new), axis=0, keepdims=True
                )
                top_ref[s] = new

        return carry

    lax.fori_loop(0, x_vmem.shape[0], step, 0)
    finish()


def col_kernel(ids_ref, cnt_ref, order_ref, f_ref, t_hbm, x_hbm, top_ref, tot_ref, t_vmem, x_vmem, t_sem, x_sem, flags, *, scale, slots, window):
    arrive, need, finish = load_all(order_ref, t_hbm, x_hbm, t_vmem, x_vmem, t_sem, x_sem, flags, window)
    top_ref[...] = jnp.full(top_ref.shape, VERY_LOW, jnp.float32)
    tot_ref[...] = jnp.zeros(tot_ref.shape, jnp.float32)

    def step(s, carry):
        arrive(s)
        for c in range(slots):

            @pl.when(c < cnt_ref[s])
            def _():
                t = ids_ref[s * slots + c]
                need(t)
                k = lax.dot_general(x_vmem[s], t_vmem[t], NT_DIMS, preferred_element_type=jnp.float32)
                logits = f_ref[s] + k * scale
                old = top_ref[t]
                new = jnp.maximum(old, jnp.max(logits, axis=0, keepdims=True))
                tot_ref[t] = tot_ref[t] * jnp.exp(old - new) + jnp.sum(
                    jnp.exp(logits - new), axis=0, keepdims=True
                )
                top_ref[t] = new

        return carry

    lax.fori_loop(0, x_vmem.shape[0], step, 0)
    finish()


def first_use_order(ids, cnt, tiles):
    blocks, slots = ids.shape
    live = jnp.arange(slots, dtype=jnp.int32)[None, :] < cnt[:, None]
    position = jnp.arange(blocks * slots, dtype=jnp.int32).reshape(blocks, slots)
    hit = (ids[:, :, None] == jnp.arange(tiles, dtype=jnp.int32)) & live[:, :, None]
    first = jnp.min(jnp.where(hit, position[:, :, None], blocks * slots), axis=(0, 1))
    return jnp.argsort(first).astype(jnp.int32)


def resident_call(body, ids, cnt, side, targets, x_all, rows, out_shape, scale):
    tiles, width, depth = targets.shape
    blocks = x_all.shape[0]
    slots = ids.shape[1]
    smem = pl.BlockSpec(memory_space=pltpu.SMEM)
    vmem = pl.BlockSpec(memory_space=pltpu.VMEM)
    hbm = pl.BlockSpec(memory_space=pl.ANY)
    cost = pl.CostEstimate(
        flops=2 * blocks * slots * rows * width * depth,
        transcendentals=blocks * slots * rows * width,
        bytes_accessed=2 * (targets.size + blocks * rows * depth),
    )
    kernel = lambda *refs: body(*refs, scale=scale, slots=slots, window=4)
    return pl.pallas_call(
        kernel,
        out_shape=(out_shape, out_shape),
        in_specs=[smem, smem, smem, vmem, hbm, hbm],
        out_specs=(vmem, vmem),
        scratch_shapes=[
            pltpu.VMEM((tiles, width, depth), targets.dtype),
            pltpu.VMEM((blocks, rows, depth), x_all.dtype),
            pltpu.SemaphoreType.DMA((tiles,)),
            pltpu.SemaphoreType.DMA((blocks,)),
            pltpu.SMEM((tiles,), jnp.int32),
        ],
        compiler_params=pltpu.CompilerParams(vmem_limit_bytes=56 * 1024 * 1024),
        cost_estimate=cost,
    )(ids.reshape(-1), cnt, first_use_order(ids, cnt, tiles), side, targets, x_all)


def local(sources, log_a, targets, g_old, log_b, tile_ids, live_count):
    tiles_own, width, depth = targets.shape
    rows = sources.shape[0]
    slots_per = tile_ids.shape[2]
    groups = tile_ids.shape[1]
    me = lax.axis_index("src")
    scale = 1.0 / (math.sqrt(depth) * EPSILON)

    meta = jnp.concatenate([tile_ids[0].reshape(-1), live_count[0].reshape(-1)])
    x_all = lax.all_gather(sources, "src")
    blocks = x_all.shape[0]
    meta_all = lax.all_to_all(
        jnp.broadcast_to(meta[None], (blocks,) + meta.shape), "src", 0, 0, tiled=True
    )
    ids_all = meta_all[:, : groups * slots_per].reshape(blocks, groups, slots_per)
    cnt_all = meta_all[:, groups * slots_per :]
    my_ids = jnp.clip(lax.dynamic_index_in_dim(ids_all, me, 1, False) - me * tiles_own, 0, tiles_own - 1)
    my_cnt = lax.dynamic_index_in_dim(cnt_all, me, 1, False)

    g_col = (g_old.astype(jnp.float32) / EPSILON)[:, :, None]
    row_top, row_total = resident_call(
        row_kernel, my_ids, my_cnt, g_col, targets, x_all, rows,
        jax.ShapeDtypeStruct((blocks, 1, rows), jnp.float32), scale,
    )
    sent = jnp.stack([row_top.reshape(blocks, rows), row_total.reshape(blocks, rows)], axis=1)
    got = lax.all_to_all(sent, "src", 0, 0, tiled=True)
    top = jnp.max(got[:, 0], axis=0)
    total = jnp.sum(got[:, 1] * jnp.exp(got[:, 0] - top[None]), axis=0)
    f_new = EPSILON * log_a - EPSILON * (top + jnp.log(total))
    f_all = lax.all_to_all(
        jnp.broadcast_to(f_new[None], (blocks,) + f_new.shape), "src", 0, 0, tiled=True
    )

    f_col = (f_all / EPSILON)[:, :, None]
    tile_top, tile_total = resident_call(
        col_kernel, my_ids, my_cnt, f_col, targets, x_all, rows,
        jax.ShapeDtypeStruct((tiles_own, 1, width), jnp.float32), scale,
    )
    col = jnp.concatenate([tile_top.reshape(tiles_own, width), tile_total.reshape(tiles_own, width)])
    loop_size = lax.axis_size("loop")
    col_all = lax.all_to_all(
        jnp.broadcast_to(col[None], (loop_size,) + col.shape), "loop", 0, 0, tiled=True
    )
    tops = col_all[:, :tiles_own]
    all_top = jnp.max(tops, axis=0)
    all_total = jnp.sum(col_all[:, tiles_own:] * jnp.exp(tops - all_top[None]), axis=0)
    g_new = EPSILON * log_b - EPSILON * (all_top + jnp.log(all_total))
    return (f_new, g_new)


def solution(mesh):
    return jax.shard_map(
        local,
        mesh=mesh,
        in_specs=(
            P(("src", "loop"), None),
            P(("src", "loop")),
            P("src", None, None),
            P("src", None),
            P("src", None),
            P(("src", "loop"), None, None),
            P(("src", "loop"), None),
        ),
        out_specs=(P(("src", "loop")), P("src", None)),
        check_vma=False,
    )
```

```python
import math

import jax
import jax.numpy as jnp
from jax import lax
from jax.experimental import pallas as pl
from jax.experimental.pallas import tpu as pltpu
from jax.sharding import PartitionSpec as P

EPSILON = 0.1
VERY_LOW = -1e30
NT_DIMS = (((1,), (1,)), ((), ()))


def load_all(order_ref, t_hbm, x_hbm, t_vmem, x_vmem, t_sem, x_sem, flags, window):
    tiles, blocks = t_vmem.shape[0], x_vmem.shape[0]
    rows = x_vmem.shape[1]

    def x_copy(s):
        return pltpu.make_async_copy(x_hbm.at[s, pl.ds(0, rows)], x_vmem.at[s], x_sem.at[s])

    def t_copy(t):
        return pltpu.make_async_copy(t_hbm.at[t], t_vmem.at[t], t_sem.at[t])

    for t in range(tiles):
        flags[t] = 0
    issue = [("x", 0), ("t", 0), ("t", 1), ("x", 1), ("t", 2), ("x", 2), ("t", 3), ("x", 3)]
    issue = [item for item in issue if item[1] < (blocks if item[0] == "x" else tiles)]
    issue += [("x", s) for s in range(4, min(window, blocks))]
    issue += [("t", k) for k in range(4, tiles)]
    for kind, k in issue:
        if kind == "x":
            x_copy(k).start()
        else:
            t_copy(order_ref[k]).start()

    def arrive(s):
        x_copy(s).wait()

        @pl.when(s + window < blocks)
        def _():
            x_copy(jnp.minimum(s + window, blocks - 1)).start()

    def need(t):
        @pl.when(flags[t] == 0)
        def _():
            t_copy(t).wait()
            flags[t] = 1

    def finish():
        for t in range(tiles):
            need(t)

    return arrive, need, finish


def row_kernel(ids_ref, cnt_ref, order_ref, g_ref, t_hbm, x_hbm, top_ref, tot_ref, t_vmem, x_vmem, t_sem, x_sem, flags, *, scale, slots, window):
    arrive, need, finish = load_all(order_ref, t_hbm, x_hbm, t_vmem, x_vmem, t_sem, x_sem, flags, window)

    def step(s, carry):
        arrive(s)
        top_ref[s] = jnp.full(top_ref.shape[1:], VERY_LOW, jnp.float32)
        tot_ref[s] = jnp.zeros(tot_ref.shape[1:], jnp.float32)
        for c in range(slots):

            @pl.when(c < cnt_ref[s])
            def _():
                t = ids_ref[s * slots + c]
                need(t)
                kt = lax.dot_general(t_vmem[t], x_vmem[s], NT_DIMS, preferred_element_type=jnp.float32)
                logits = g_ref[t] + kt * scale
                old = top_ref[s]
                new = jnp.maximum(old, jnp.max(logits, axis=0, keepdims=True))
                tot_ref[s] = tot_ref[s] * jnp.exp(old - new) + jnp.sum(
                    jnp.exp(logits - new), axis=0, keepdims=True
                )
                top_ref[s] = new

        return carry

    lax.fori_loop(0, x_vmem.shape[0], step, 0)
    finish()


def col_kernel(ids_ref, cnt_ref, order_ref, f_ref, t_hbm, x_hbm, top_ref, tot_ref, t_vmem, x_vmem, t_sem, x_sem, flags, *, scale, slots, window):
    arrive, need, finish = load_all(order_ref, t_hbm, x_hbm, t_vmem, x_vmem, t_sem, x_sem, flags, window)
    top_ref[...] = jnp.full(top_ref.shape, VERY_LOW, jnp.float32)
    tot_ref[...] = jnp.zeros(tot_ref.shape, jnp.float32)

    def step(s, carry):
        arrive(s)
        f_row = f_ref[s]
        f_column = jnp.transpose(jnp.broadcast_to(f_row, (128, f_row.shape[1])))[:, :1]
        for c in range(slots):

            @pl.when(c < cnt_ref[s])
            def _():
                t = ids_ref[s * slots + c]
                need(t)
                k = lax.dot_general(x_vmem[s], t_vmem[t], NT_DIMS, preferred_element_type=jnp.float32)
                logits = f_column + k * scale
                old = top_ref[t]
                new = jnp.maximum(old, jnp.max(logits, axis=0, keepdims=True))
                tot_ref[t] = tot_ref[t] * jnp.exp(old - new) + jnp.sum(
                    jnp.exp(logits - new), axis=0, keepdims=True
                )
                top_ref[t] = new

        return carry

    lax.fori_loop(0, x_vmem.shape[0], step, 0)
    finish()


def first_use_order(ids, cnt, tiles):
    blocks, slots = ids.shape
    live = jnp.arange(slots, dtype=jnp.int32)[None, :] < cnt[:, None]
    position = jnp.arange(blocks * slots, dtype=jnp.int32).reshape(blocks, slots)
    hit = (ids[:, :, None] == jnp.arange(tiles, dtype=jnp.int32)) & live[:, :, None]
    first = jnp.min(jnp.where(hit, position[:, :, None], blocks * slots), axis=(0, 1))
    return jnp.argsort(first).astype(jnp.int32)


def resident_call(body, ids, cnt, side, targets, x_all, rows, out_shape, scale):
    tiles, width, depth = targets.shape
    blocks = x_all.shape[0]
    slots = ids.shape[1]
    smem = pl.BlockSpec(memory_space=pltpu.SMEM)
    vmem = pl.BlockSpec(memory_space=pltpu.VMEM)
    hbm = pl.BlockSpec(memory_space=pl.ANY)
    cost = pl.CostEstimate(
        flops=2 * blocks * slots * rows * width * depth,
        transcendentals=blocks * slots * rows * width,
        bytes_accessed=2 * (targets.size + blocks * rows * depth),
    )
    kernel = lambda *refs: body(*refs, scale=scale, slots=slots, window=4)
    return pl.pallas_call(
        kernel,
        out_shape=(out_shape, out_shape),
        in_specs=[smem, smem, smem, vmem, hbm, hbm],
        out_specs=(vmem, vmem),
        scratch_shapes=[
            pltpu.VMEM((tiles, width, depth), targets.dtype),
            pltpu.VMEM((blocks, rows, depth), x_all.dtype),
            pltpu.SemaphoreType.DMA((tiles,)),
            pltpu.SemaphoreType.DMA((blocks,)),
            pltpu.SMEM((tiles,), jnp.int32),
        ],
        compiler_params=pltpu.CompilerParams(vmem_limit_bytes=56 * 1024 * 1024),
        cost_estimate=cost,
    )(ids.reshape(-1), cnt, first_use_order(ids, cnt, tiles), side, targets, x_all)


def local(sources, log_a, targets, g_old, log_b, tile_ids, live_count):
    tiles_own, width, depth = targets.shape
    rows = sources.shape[0]
    slots_per = tile_ids.shape[2]
    groups = tile_ids.shape[1]
    me = lax.axis_index("src")
    scale = 1.0 / (math.sqrt(depth) * EPSILON)

    meta = jnp.concatenate([tile_ids[0].reshape(-1), live_count[0].reshape(-1)])
    x_all = lax.all_gather(sources, "src")
    blocks = x_all.shape[0]
    meta_all = lax.all_to_all(
        jnp.broadcast_to(meta[None], (blocks,) + meta.shape), "src", 0, 0, tiled=True
    )
    ids_all = meta_all[:, : groups * slots_per].reshape(blocks, groups, slots_per)
    cnt_all = meta_all[:, groups * slots_per :]
    my_ids = jnp.clip(lax.dynamic_index_in_dim(ids_all, me, 1, False) - me * tiles_own, 0, tiles_own - 1)
    my_cnt = lax.dynamic_index_in_dim(cnt_all, me, 1, False)

    g_col = (g_old.astype(jnp.float32) / EPSILON)[:, :, None]
    row_top, row_total = resident_call(
        row_kernel, my_ids, my_cnt, g_col, targets, x_all, rows,
        jax.ShapeDtypeStruct((blocks, 1, rows), jnp.float32), scale,
    )
    sent = jnp.stack([row_top.reshape(blocks, rows), row_total.reshape(blocks, rows)], axis=1)
    got = lax.all_to_all(sent, "src", 0, 0, tiled=True)
    top = jnp.max(got[:, 0], axis=0)
    total = jnp.sum(got[:, 1] * jnp.exp(got[:, 0] - top[None]), axis=0)
    f_new = EPSILON * log_a - EPSILON * (top + jnp.log(total))
    f_all = lax.all_to_all(
        jnp.broadcast_to(f_new[None], (blocks,) + f_new.shape), "src", 0, 0, tiled=True
    )

    f_col = (f_all / EPSILON)[:, None, :]
    tile_top, tile_total = resident_call(
        col_kernel, my_ids, my_cnt, f_col, targets, x_all, rows,
        jax.ShapeDtypeStruct((tiles_own, 1, width), jnp.float32), scale,
    )
    col = jnp.concatenate([tile_top.reshape(tiles_own, width), tile_total.reshape(tiles_own, width)])
    loop_size = lax.axis_size("loop")
    col_all = lax.all_to_all(
        jnp.broadcast_to(col[None], (loop_size,) + col.shape), "loop", 0, 0, tiled=True
    )
    tops = col_all[:, :tiles_own]
    all_top = jnp.max(tops, axis=0)
    all_total = jnp.sum(col_all[:, tiles_own:] * jnp.exp(tops - all_top[None]), axis=0)
    g_new = EPSILON * log_b - EPSILON * (all_top + jnp.log(all_total))
    return (f_new, g_new)


def solution(mesh):
    return jax.shard_map(
        local,
        mesh=mesh,
        in_specs=(
            P(("src", "loop"), None),
            P(("src", "loop")),
            P("src", None, None),
            P("src", None),
            P("src", None),
            P(("src", "loop"), None, None),
            P(("src", "loop"), None),
        ),
        out_specs=(P(("src", "loop")), P("src", None)),
        check_vma=False,
    )
```

```python
import math

import jax
import jax.numpy as jnp
from jax import lax
from jax.experimental import pallas as pl
from jax.experimental.pallas import tpu as pltpu
from jax.sharding import PartitionSpec as P

EPSILON = 0.1
VERY_LOW = -1e30
NT_DIMS = (((1,), (1,)), ((), ()))


def load_all(order_ref, t_hbm, x_hbm, t_vmem, x_vmem, t_sem, x_sem, flags, window):
    tiles, blocks = t_vmem.shape[0], x_vmem.shape[0]
    rows = x_vmem.shape[1]

    def x_copy(s):
        return pltpu.make_async_copy(x_hbm.at[s, pl.ds(0, rows)], x_vmem.at[s], x_sem.at[s])

    def t_copy(t):
        return pltpu.make_async_copy(t_hbm.at[t], t_vmem.at[t], t_sem.at[t])

    for t in range(tiles):
        flags[t] = 0
    issue = [("x", 0), ("t", 0), ("t", 1), ("x", 1), ("t", 2), ("x", 2), ("t", 3), ("x", 3)]
    issue = [item for item in issue if item[1] < (min(window, blocks) if item[0] == "x" else tiles)]
    issue += [("x", s) for s in range(4, min(window, blocks))]
    issue += [("t", k) for k in range(4, tiles)]
    for kind, k in issue:
        if kind == "x":
            x_copy(k).start()
        else:
            t_copy(order_ref[k]).start()

    def arrive(s):
        x_copy(s).wait()

        @pl.when(s + window < blocks)
        def _():
            x_copy(jnp.minimum(s + window, blocks - 1)).start()

    def need(t):
        @pl.when(flags[t] == 0)
        def _():
            t_copy(t).wait()
            flags[t] = 1

    def finish():
        for t in range(tiles):
            need(t)

    return arrive, need, finish


def row_kernel(ids_ref, cnt_ref, order_ref, g_ref, t_hbm, x_hbm, top_ref, tot_ref, t_vmem, x_vmem, t_sem, x_sem, flags, *, scale, slots, window):
    arrive, need, finish = load_all(order_ref, t_hbm, x_hbm, t_vmem, x_vmem, t_sem, x_sem, flags, window)

    def step(s, carry):
        arrive(s)
        top_ref[s] = jnp.full(top_ref.shape[1:], VERY_LOW, jnp.float32)
        tot_ref[s] = jnp.zeros(tot_ref.shape[1:], jnp.float32)
        for c in range(slots):

            @pl.when(c < cnt_ref[s])
            def _():
                t = ids_ref[s * slots + c]
                need(t)
                kt = lax.dot_general(t_vmem[t], x_vmem[s], NT_DIMS, preferred_element_type=jnp.float32)
                logits = g_ref[t] + kt * scale
                old = top_ref[s]
                new = jnp.maximum(old, jnp.max(logits, axis=0, keepdims=True))
                tot_ref[s] = tot_ref[s] * jnp.exp(old - new) + jnp.sum(
                    jnp.exp(logits - new), axis=0, keepdims=True
                )
                top_ref[s] = new

        return carry

    lax.fori_loop(0, x_vmem.shape[0], step, 0)
    finish()


def col_kernel(ids_ref, cnt_ref, order_ref, f_ref, t_hbm, x_hbm, top_ref, tot_ref, t_vmem, x_vmem, t_sem, x_sem, flags, *, scale, slots, window):
    arrive, need, finish = load_all(order_ref, t_hbm, x_hbm, t_vmem, x_vmem, t_sem, x_sem, flags, window)
    top_ref[...] = jnp.full(top_ref.shape, VERY_LOW, jnp.float32)
    tot_ref[...] = jnp.zeros(tot_ref.shape, jnp.float32)

    def step(s, carry):
        arrive(s)
        f_row = f_ref[s]
        f_column = jnp.transpose(jnp.broadcast_to(f_row, (128, f_row.shape[1])))[:, :1]
        for c in range(slots):

            @pl.when(c < cnt_ref[s])
            def _():
                t = ids_ref[s * slots + c]
                need(t)
                k = lax.dot_general(x_vmem[s], t_vmem[t], NT_DIMS, preferred_element_type=jnp.float32)
                logits = f_column + k * scale
                old = top_ref[t]
                new = jnp.maximum(old, jnp.max(logits, axis=0, keepdims=True))
                tot_ref[t] = tot_ref[t] * jnp.exp(old - new) + jnp.sum(
                    jnp.exp(logits - new), axis=0, keepdims=True
                )
                top_ref[t] = new

        return carry

    lax.fori_loop(0, x_vmem.shape[0], step, 0)
    finish()


def first_use_order(ids, cnt, tiles):
    blocks, slots = ids.shape
    live = jnp.arange(slots, dtype=jnp.int32)[None, :] < cnt[:, None]
    position = jnp.arange(blocks * slots, dtype=jnp.int32).reshape(blocks, slots)
    hit = (ids[:, :, None] == jnp.arange(tiles, dtype=jnp.int32)) & live[:, :, None]
    first = jnp.min(jnp.where(hit, position[:, :, None], blocks * slots), axis=(0, 1))
    return jnp.argsort(first).astype(jnp.int32)


def resident_call(body, ids, cnt, side, targets, x_all, rows, out_shape, scale):
    tiles, width, depth = targets.shape
    blocks = x_all.shape[0]
    slots = ids.shape[1]
    smem = pl.BlockSpec(memory_space=pltpu.SMEM)
    vmem = pl.BlockSpec(memory_space=pltpu.VMEM)
    hbm = pl.BlockSpec(memory_space=pl.ANY)
    cost = pl.CostEstimate(
        flops=2 * blocks * slots * rows * width * depth,
        transcendentals=blocks * slots * rows * width,
        bytes_accessed=2 * (targets.size + blocks * rows * depth),
    )
    kernel = lambda *refs: body(*refs, scale=scale, slots=slots, window=2)
    return pl.pallas_call(
        kernel,
        out_shape=(out_shape, out_shape),
        in_specs=[smem, smem, smem, vmem, hbm, hbm],
        out_specs=(vmem, vmem),
        scratch_shapes=[
            pltpu.VMEM((tiles, width, depth), targets.dtype),
            pltpu.VMEM((blocks, rows, depth), x_all.dtype),
            pltpu.SemaphoreType.DMA((tiles,)),
            pltpu.SemaphoreType.DMA((blocks,)),
            pltpu.SMEM((tiles,), jnp.int32),
        ],
        compiler_params=pltpu.CompilerParams(vmem_limit_bytes=56 * 1024 * 1024),
        cost_estimate=cost,
    )(ids.reshape(-1), cnt, first_use_order(ids, cnt, tiles), side, targets, x_all)


def local(sources, log_a, targets, g_old, log_b, tile_ids, live_count):
    tiles_own, width, depth = targets.shape
    rows = sources.shape[0]
    slots_per = tile_ids.shape[2]
    groups = tile_ids.shape[1]
    me = lax.axis_index("src")
    scale = 1.0 / (math.sqrt(depth) * EPSILON)

    meta = jnp.concatenate([tile_ids[0].reshape(-1), live_count[0].reshape(-1)])
    x_all = lax.all_gather(sources, "src")
    blocks = x_all.shape[0]
    meta_all = lax.all_to_all(
        jnp.broadcast_to(meta[None], (blocks,) + meta.shape), "src", 0, 0, tiled=True
    )
    ids_all = meta_all[:, : groups * slots_per].reshape(blocks, groups, slots_per)
    cnt_all = meta_all[:, groups * slots_per :]
    my_ids = jnp.clip(lax.dynamic_index_in_dim(ids_all, me, 1, False) - me * tiles_own, 0, tiles_own - 1)
    my_cnt = lax.dynamic_index_in_dim(cnt_all, me, 1, False)

    g_col = (g_old.astype(jnp.float32) / EPSILON)[:, :, None]
    row_top, row_total = resident_call(
        row_kernel, my_ids, my_cnt, g_col, targets, x_all, rows,
        jax.ShapeDtypeStruct((blocks, 1, rows), jnp.float32), scale,
    )
    sent = jnp.stack([row_top.reshape(blocks, rows), row_total.reshape(blocks, rows)], axis=1)
    got = lax.all_to_all(sent, "src", 0, 0, tiled=True)
    top = jnp.max(got[:, 0], axis=0)
    total = jnp.sum(got[:, 1] * jnp.exp(got[:, 0] - top[None]), axis=0)
    f_new = EPSILON * log_a - EPSILON * (top + jnp.log(total))
    f_all = lax.all_to_all(
        jnp.broadcast_to(f_new[None], (blocks,) + f_new.shape), "src", 0, 0, tiled=True
    )

    f_col = (f_all / EPSILON)[:, None, :]
    tile_top, tile_total = resident_call(
        col_kernel, my_ids, my_cnt, f_col, targets, x_all, rows,
        jax.ShapeDtypeStruct((tiles_own, 1, width), jnp.float32), scale,
    )
    col = jnp.concatenate([tile_top.reshape(tiles_own, width), tile_total.reshape(tiles_own, width)])
    loop_size = lax.axis_size("loop")
    col_all = lax.all_to_all(
        jnp.broadcast_to(col[None], (loop_size,) + col.shape), "loop", 0, 0, tiled=True
    )
    tops = col_all[:, :tiles_own]
    all_top = jnp.max(tops, axis=0)
    all_total = jnp.sum(col_all[:, tiles_own:] * jnp.exp(tops - all_top[None]), axis=0)
    g_new = EPSILON * log_b - EPSILON * (all_top + jnp.log(all_total))
    return (f_new, g_new)


def solution(mesh):
    return jax.shard_map(
        local,
        mesh=mesh,
        in_specs=(
            P(("src", "loop"), None),
            P(("src", "loop")),
            P("src", None, None),
            P("src", None),
            P("src", None),
            P(("src", "loop"), None, None),
            P(("src", "loop"), None),
        ),
        out_specs=(P(("src", "loop")), P("src", None)),
        check_vma=False,
    )
```

```python
import math

import jax
import jax.numpy as jnp
from jax import lax
from jax.experimental import pallas as pl
from jax.experimental.pallas import tpu as pltpu
from jax.sharding import PartitionSpec as P

EPSILON = 0.1
VERY_LOW = -1e30
NT_DIMS = (((1,), (1,)), ((), ()))


def load_all(order_ref, t_hbm, x_hbm, t_vmem, x_vmem, t_sem, x_sem, flags, window):
    tiles, blocks = t_vmem.shape[0], x_vmem.shape[0]
    rows = x_vmem.shape[1]

    def x_copy(s):
        return pltpu.make_async_copy(x_hbm.at[s, pl.ds(0, rows)], x_vmem.at[s], x_sem.at[s])

    def t_copy(t):
        return pltpu.make_async_copy(t_hbm.at[t], t_vmem.at[t], t_sem.at[t])

    for t in range(tiles):
        flags[t] = 0
    issue = [("x", 0), ("t", 0), ("t", 1), ("x", 1), ("t", 2), ("x", 2), ("t", 3), ("x", 3)]
    issue = [item for item in issue if item[1] < (min(window, blocks) if item[0] == "x" else tiles)]
    issue += [("x", s) for s in range(4, min(window, blocks))]
    issue += [("t", k) for k in range(4, tiles)]
    for kind, k in issue:
        if kind == "x":
            x_copy(k).start()
        else:
            t_copy(order_ref[k]).start()

    def arrive(s):
        x_copy(s).wait()

        @pl.when(s + window < blocks)
        def _():
            x_copy(jnp.minimum(s + window, blocks - 1)).start()

    def need(t):
        @pl.when(flags[t] == 0)
        def _():
            t_copy(t).wait()
            flags[t] = 1

    def finish():
        for t in range(tiles):
            need(t)

    return arrive, need, finish


def row_kernel(ids_ref, cnt_ref, order_ref, g_ref, t_hbm, x_hbm, top_ref, tot_ref, t_vmem, x_vmem, t_sem, x_sem, flags, *, scale, slots, window):
    arrive, need, finish = load_all(order_ref, t_hbm, x_hbm, t_vmem, x_vmem, t_sem, x_sem, flags, window)

    def step(s, carry):
        arrive(s)
        top_ref[s] = jnp.full(top_ref.shape[1:], VERY_LOW, jnp.float32)
        tot_ref[s] = jnp.zeros(tot_ref.shape[1:], jnp.float32)
        for c in range(slots):

            @pl.when(c < cnt_ref[s])
            def _():
                t = ids_ref[s * slots + c]
                need(t)
                kt = lax.dot_general(t_vmem[t], x_vmem[s], NT_DIMS, preferred_element_type=jnp.float32)
                logits = g_ref[t] + kt * scale
                old = top_ref[s]
                new = jnp.maximum(old, jnp.max(logits, axis=0, keepdims=True))
                tot_ref[s] = tot_ref[s] * jnp.exp(old - new) + jnp.sum(
                    jnp.exp(logits - new), axis=0, keepdims=True
                )
                top_ref[s] = new

        return carry

    lax.fori_loop(0, x_vmem.shape[0], step, 0)
    finish()


def col_kernel(ids_ref, cnt_ref, order_ref, f_ref, t_hbm, x_hbm, top_ref, tot_ref, t_vmem, x_vmem, t_sem, x_sem, flags, *, scale, slots, window):
    arrive, need, finish = load_all(order_ref, t_hbm, x_hbm, t_vmem, x_vmem, t_sem, x_sem, flags, window)
    top_ref[...] = jnp.full(top_ref.shape, VERY_LOW, jnp.float32)
    tot_ref[...] = jnp.zeros(tot_ref.shape, jnp.float32)

    def step(s, carry):
        arrive(s)
        f_row = f_ref[s]
        f_column = jnp.transpose(jnp.broadcast_to(f_row, (128, f_row.shape[1])))[:, :1]
        for c in range(slots):

            @pl.when(c < cnt_ref[s])
            def _():
                t = ids_ref[s * slots + c]
                need(t)
                k = lax.dot_general(x_vmem[s], t_vmem[t], NT_DIMS, preferred_element_type=jnp.float32)
                logits = f_column + k * scale
                old = top_ref[t]
                new = jnp.maximum(old, jnp.max(logits, axis=0, keepdims=True))
                tot_ref[t] = tot_ref[t] * jnp.exp(old - new) + jnp.sum(
                    jnp.exp(logits - new), axis=0, keepdims=True
                )
                top_ref[t] = new

        return carry

    lax.fori_loop(0, x_vmem.shape[0], step, 0)
    finish()


def first_use_order(ids, cnt, tiles):
    blocks, slots = ids.shape
    live = jnp.arange(slots, dtype=jnp.int32)[None, :] < cnt[:, None]
    position = jnp.arange(blocks * slots, dtype=jnp.int32).reshape(blocks, slots)
    hit = (ids[:, :, None] == jnp.arange(tiles, dtype=jnp.int32)) & live[:, :, None]
    first = jnp.min(jnp.where(hit, position[:, :, None], blocks * slots), axis=(0, 1))
    return jnp.argsort(first).astype(jnp.int32)


def resident_call(body, ids, cnt, side, targets, x_all, rows, out_shape, scale):
    tiles, width, depth = targets.shape
    blocks = x_all.shape[0]
    slots = ids.shape[1]
    smem = pl.BlockSpec(memory_space=pltpu.SMEM)
    vmem = pl.BlockSpec(memory_space=pltpu.VMEM)
    hbm = pl.BlockSpec(memory_space=pl.ANY)
    cost = pl.CostEstimate(
        flops=2 * blocks * slots * rows * width * depth,
        transcendentals=blocks * slots * rows * width,
        bytes_accessed=2 * (targets.size + blocks * rows * depth),
    )
    kernel = lambda *refs: body(*refs, scale=scale, slots=slots, window=6)
    return pl.pallas_call(
        kernel,
        out_shape=(out_shape, out_shape),
        in_specs=[smem, smem, smem, vmem, hbm, hbm],
        out_specs=(vmem, vmem),
        scratch_shapes=[
            pltpu.VMEM((tiles, width, depth), targets.dtype),
            pltpu.VMEM((blocks, rows, depth), x_all.dtype),
            pltpu.SemaphoreType.DMA((tiles,)),
            pltpu.SemaphoreType.DMA((blocks,)),
            pltpu.SMEM((tiles,), jnp.int32),
        ],
        compiler_params=pltpu.CompilerParams(vmem_limit_bytes=56 * 1024 * 1024),
        cost_estimate=cost,
    )(ids.reshape(-1), cnt, first_use_order(ids, cnt, tiles), side, targets, x_all)


def local(sources, log_a, targets, g_old, log_b, tile_ids, live_count):
    tiles_own, width, depth = targets.shape
    rows = sources.shape[0]
    slots_per = tile_ids.shape[2]
    groups = tile_ids.shape[1]
    me = lax.axis_index("src")
    scale = 1.0 / (math.sqrt(depth) * EPSILON)

    meta = jnp.concatenate([tile_ids[0].reshape(-1), live_count[0].reshape(-1)])
    x_all = lax.all_gather(sources, "src")
    blocks = x_all.shape[0]
    meta_all = lax.all_to_all(
        jnp.broadcast_to(meta[None], (blocks,) + meta.shape), "src", 0, 0, tiled=True
    )
    ids_all = meta_all[:, : groups * slots_per].reshape(blocks, groups, slots_per)
    cnt_all = meta_all[:, groups * slots_per :]
    my_ids = jnp.clip(lax.dynamic_index_in_dim(ids_all, me, 1, False) - me * tiles_own, 0, tiles_own - 1)
    my_cnt = lax.dynamic_index_in_dim(cnt_all, me, 1, False)

    g_col = (g_old.astype(jnp.float32) / EPSILON)[:, :, None]
    row_top, row_total = resident_call(
        row_kernel, my_ids, my_cnt, g_col, targets, x_all, rows,
        jax.ShapeDtypeStruct((blocks, 1, rows), jnp.float32), scale,
    )
    sent = jnp.stack([row_top.reshape(blocks, rows), row_total.reshape(blocks, rows)], axis=1)
    got = lax.all_to_all(sent, "src", 0, 0, tiled=True)
    top = jnp.max(got[:, 0], axis=0)
    total = jnp.sum(got[:, 1] * jnp.exp(got[:, 0] - top[None]), axis=0)
    f_new = EPSILON * log_a - EPSILON * (top + jnp.log(total))
    f_all = lax.all_to_all(
        jnp.broadcast_to(f_new[None], (blocks,) + f_new.shape), "src", 0, 0, tiled=True
    )

    f_col = (f_all / EPSILON)[:, None, :]
    tile_top, tile_total = resident_call(
        col_kernel, my_ids, my_cnt, f_col, targets, x_all, rows,
        jax.ShapeDtypeStruct((tiles_own, 1, width), jnp.float32), scale,
    )
    col = jnp.concatenate([tile_top.reshape(tiles_own, width), tile_total.reshape(tiles_own, width)])
    loop_size = lax.axis_size("loop")
    col_all = lax.all_to_all(
        jnp.broadcast_to(col[None], (loop_size,) + col.shape), "loop", 0, 0, tiled=True
    )
    tops = col_all[:, :tiles_own]
    all_top = jnp.max(tops, axis=0)
    all_total = jnp.sum(col_all[:, tiles_own:] * jnp.exp(tops - all_top[None]), axis=0)
    g_new = EPSILON * log_b - EPSILON * (all_top + jnp.log(all_total))
    return (f_new, g_new)


def solution(mesh):
    return jax.shard_map(
        local,
        mesh=mesh,
        in_specs=(
            P(("src", "loop"), None),
            P(("src", "loop")),
            P("src", None, None),
            P("src", None),
            P("src", None),
            P(("src", "loop"), None, None),
            P(("src", "loop"), None),
        ),
        out_specs=(P(("src", "loop")), P("src", None)),
        check_vma=False,
    )
```

```python
import math

import jax
import jax.numpy as jnp
from jax import lax
from jax.experimental import pallas as pl
from jax.experimental.pallas import tpu as pltpu
from jax.sharding import PartitionSpec as P

EPSILON = 0.1
VERY_LOW = -1e30
NT_DIMS = (((1,), (1,)), ((), ()))


def load_all(order_ref, t_hbm, x_hbm, t_vmem, x_vmem, t_sem, x_sem, flags, window):
    tiles, blocks = t_vmem.shape[0], x_vmem.shape[0]
    rows = x_vmem.shape[1]

    def x_copy(s):
        return pltpu.make_async_copy(x_hbm.at[s, pl.ds(0, rows)], x_vmem.at[s], x_sem.at[s])

    def t_copy(t):
        return pltpu.make_async_copy(t_hbm.at[t], t_vmem.at[t], t_sem.at[t])

    for t in range(tiles):
        flags[t] = 0
    issue = [("x", 0), ("t", 0), ("t", 1), ("x", 1), ("t", 2), ("x", 2), ("t", 3), ("x", 3)]
    issue = [item for item in issue if item[1] < (min(window, blocks) if item[0] == "x" else tiles)]
    issue += [("x", s) for s in range(4, min(window, blocks))]
    issue += [("t", k) for k in range(4, tiles)]
    for kind, k in issue:
        if kind == "x":
            x_copy(k).start()
        else:
            t_copy(order_ref[k]).start()

    def arrive(s):
        x_copy(s).wait()

        @pl.when(s + window < blocks)
        def _():
            x_copy(jnp.minimum(s + window, blocks - 1)).start()

    def need(t):
        @pl.when(flags[t] == 0)
        def _():
            t_copy(t).wait()
            flags[t] = 1

    def finish():
        for t in range(tiles):
            need(t)

    return arrive, need, finish


def row_kernel(ids_ref, cnt_ref, order_ref, g_ref, t_hbm, x_hbm, top_ref, tot_ref, t_vmem, x_vmem, t_sem, x_sem, flags, *, scale, slots, window):
    arrive, need, finish = load_all(order_ref, t_hbm, x_hbm, t_vmem, x_vmem, t_sem, x_sem, flags, window)

    def step(s, carry):
        arrive(s)
        top_ref[s] = jnp.full(top_ref.shape[1:], VERY_LOW, jnp.float32)
        tot_ref[s] = jnp.zeros(tot_ref.shape[1:], jnp.float32)
        for c in range(slots):

            @pl.when(c < cnt_ref[s])
            def _():
                t = ids_ref[s * slots + c]
                need(t)
                kt = lax.dot_general(t_vmem[t], x_vmem[s], NT_DIMS, preferred_element_type=jnp.float32)
                logits = g_ref[t] + kt * scale
                old = top_ref[s]
                new = jnp.maximum(old, jnp.max(logits, axis=0, keepdims=True))
                tot_ref[s] = tot_ref[s] * jnp.exp(old - new) + jnp.sum(
                    jnp.exp(logits - new), axis=0, keepdims=True
                )
                top_ref[s] = new

        return carry

    lax.fori_loop(0, x_vmem.shape[0], step, 0)
    finish()


def col_kernel(ids_ref, cnt_ref, order_ref, f_ref, t_hbm, x_hbm, top_ref, tot_ref, t_vmem, x_vmem, t_sem, x_sem, flags, *, scale, slots, window):
    arrive, need, finish = load_all(order_ref, t_hbm, x_hbm, t_vmem, x_vmem, t_sem, x_sem, flags, window)
    top_ref[...] = jnp.full(top_ref.shape, VERY_LOW, jnp.float32)
    tot_ref[...] = jnp.zeros(tot_ref.shape, jnp.float32)

    def step(s, carry):
        arrive(s)
        f_row = f_ref[s]
        f_column = jnp.transpose(jnp.broadcast_to(f_row, (128, f_row.shape[1])))[:, :1]
        for c in range(slots):

            @pl.when(c < cnt_ref[s])
            def _():
                t = ids_ref[s * slots + c]
                need(t)
                k = lax.dot_general(x_vmem[s], t_vmem[t], NT_DIMS, preferred_element_type=jnp.float32)
                logits = f_column + k * scale
                old = top_ref[t]
                new = jnp.maximum(old, jnp.max(logits, axis=0, keepdims=True))
                tot_ref[t] = tot_ref[t] * jnp.exp(old - new) + jnp.sum(
                    jnp.exp(logits - new), axis=0, keepdims=True
                )
                top_ref[t] = new

        return carry

    lax.fori_loop(0, x_vmem.shape[0], step, 0)
    finish()


def first_use_order(ids, cnt, tiles):
    blocks, slots = ids.shape
    live = jnp.arange(slots, dtype=jnp.int32)[None, :] < cnt[:, None]
    position = jnp.arange(blocks * slots, dtype=jnp.int32).reshape(blocks, slots)
    hit = (ids[:, :, None] == jnp.arange(tiles, dtype=jnp.int32)) & live[:, :, None]
    first = jnp.min(jnp.where(hit, position[:, :, None], blocks * slots), axis=(0, 1))
    return jnp.argsort(first).astype(jnp.int32)


def resident_call(body, ids, cnt, side, targets, x_all, rows, out_shape, scale):
    tiles, width, depth = targets.shape
    blocks = x_all.shape[0]
    slots = ids.shape[1]
    smem = pl.BlockSpec(memory_space=pltpu.SMEM)
    vmem = pl.BlockSpec(memory_space=pltpu.VMEM)
    hbm = pl.BlockSpec(memory_space=pl.ANY)
    cost = pl.CostEstimate(
        flops=2 * blocks * slots * rows * width * depth,
        transcendentals=blocks * slots * rows * width,
        bytes_accessed=2 * (targets.size + blocks * rows * depth),
    )
    kernel = lambda *refs: body(*refs, scale=scale, slots=slots, window=8)
    return pl.pallas_call(
        kernel,
        out_shape=(out_shape, out_shape),
        in_specs=[smem, smem, smem, vmem, hbm, hbm],
        out_specs=(vmem, vmem),
        scratch_shapes=[
            pltpu.VMEM((tiles, width, depth), targets.dtype),
            pltpu.VMEM((blocks, rows, depth), x_all.dtype),
            pltpu.SemaphoreType.DMA((tiles,)),
            pltpu.SemaphoreType.DMA((blocks,)),
            pltpu.SMEM((tiles,), jnp.int32),
        ],
        compiler_params=pltpu.CompilerParams(vmem_limit_bytes=56 * 1024 * 1024),
        cost_estimate=cost,
    )(ids.reshape(-1), cnt, first_use_order(ids, cnt, tiles), side, targets, x_all)


def local(sources, log_a, targets, g_old, log_b, tile_ids, live_count):
    tiles_own, width, depth = targets.shape
    rows = sources.shape[0]
    slots_per = tile_ids.shape[2]
    groups = tile_ids.shape[1]
    me = lax.axis_index("src")
    scale = 1.0 / (math.sqrt(depth) * EPSILON)

    meta = jnp.concatenate([tile_ids[0].reshape(-1), live_count[0].reshape(-1)])
    x_all = lax.all_gather(sources, "src")
    blocks = x_all.shape[0]
    meta_all = lax.all_to_all(
        jnp.broadcast_to(meta[None], (blocks,) + meta.shape), "src", 0, 0, tiled=True
    )
    ids_all = meta_all[:, : groups * slots_per].reshape(blocks, groups, slots_per)
    cnt_all = meta_all[:, groups * slots_per :]
    my_ids = jnp.clip(lax.dynamic_index_in_dim(ids_all, me, 1, False) - me * tiles_own, 0, tiles_own - 1)
    my_cnt = lax.dynamic_index_in_dim(cnt_all, me, 1, False)

    g_col = (g_old.astype(jnp.float32) / EPSILON)[:, :, None]
    row_top, row_total = resident_call(
        row_kernel, my_ids, my_cnt, g_col, targets, x_all, rows,
        jax.ShapeDtypeStruct((blocks, 1, rows), jnp.float32), scale,
    )
    sent = jnp.stack([row_top.reshape(blocks, rows), row_total.reshape(blocks, rows)], axis=1)
    got = lax.all_to_all(sent, "src", 0, 0, tiled=True)
    top = jnp.max(got[:, 0], axis=0)
    total = jnp.sum(got[:, 1] * jnp.exp(got[:, 0] - top[None]), axis=0)
    f_new = EPSILON * log_a - EPSILON * (top + jnp.log(total))
    f_all = lax.all_to_all(
        jnp.broadcast_to(f_new[None], (blocks,) + f_new.shape), "src", 0, 0, tiled=True
    )

    f_col = (f_all / EPSILON)[:, None, :]
    tile_top, tile_total = resident_call(
        col_kernel, my_ids, my_cnt, f_col, targets, x_all, rows,
        jax.ShapeDtypeStruct((tiles_own, 1, width), jnp.float32), scale,
    )
    col = jnp.concatenate([tile_top.reshape(tiles_own, width), tile_total.reshape(tiles_own, width)])
    loop_size = lax.axis_size("loop")
    col_all = lax.all_to_all(
        jnp.broadcast_to(col[None], (loop_size,) + col.shape), "loop", 0, 0, tiled=True
    )
    tops = col_all[:, :tiles_own]
    all_top = jnp.max(tops, axis=0)
    all_total = jnp.sum(col_all[:, tiles_own:] * jnp.exp(tops - all_top[None]), axis=0)
    g_new = EPSILON * log_b - EPSILON * (all_top + jnp.log(all_total))
    return (f_new, g_new)


def solution(mesh):
    return jax.shard_map(
        local,
        mesh=mesh,
        in_specs=(
            P(("src", "loop"), None),
            P(("src", "loop")),
            P("src", None, None),
            P("src", None),
            P("src", None),
            P(("src", "loop"), None, None),
            P(("src", "loop"), None),
        ),
        out_specs=(P(("src", "loop")), P("src", None)),
        check_vma=False,
    )
```

```python
import math

import jax
import jax.numpy as jnp
from jax import lax
from jax.experimental import pallas as pl
from jax.experimental.pallas import tpu as pltpu
from jax.sharding import PartitionSpec as P

EPSILON = 0.1
VERY_LOW = -1e30
NT_DIMS = (((1,), (1,)), ((), ()))


def load_all(order_ref, t_hbm, x_hbm, t_vmem, x_vmem, t_sem, x_sem, flags, window):
    tiles, blocks = t_vmem.shape[0], x_vmem.shape[0]
    rows = x_vmem.shape[1]

    def x_copy(s):
        return pltpu.make_async_copy(x_hbm.at[s, pl.ds(0, rows)], x_vmem.at[s], x_sem.at[s])

    def t_copy(t):
        return pltpu.make_async_copy(t_hbm.at[t], t_vmem.at[t], t_sem.at[t])

    for t in range(tiles):
        flags[t] = 0
    issue = [("x", 0), ("t", 0), ("t", 1), ("x", 1), ("t", 2), ("x", 2), ("t", 3), ("x", 3)]
    issue = [item for item in issue if item[1] < (min(window, blocks) if item[0] == "x" else tiles)]
    issue += [("x", s) for s in range(4, min(window, blocks))]
    issue += [("t", k) for k in range(4, tiles)]
    for kind, k in issue:
        if kind == "x":
            x_copy(k).start()
        else:
            t_copy(order_ref[k]).start()

    def arrive(s):
        x_copy(s).wait()

        @pl.when(s + window < blocks)
        def _():
            x_copy(jnp.minimum(s + window, blocks - 1)).start()

    def need(t):
        @pl.when(flags[t] == 0)
        def _():
            t_copy(t).wait()
            flags[t] = 1

    def finish():
        for t in range(tiles):
            need(t)

    return arrive, need, finish


def row_kernel(ids_ref, cnt_ref, order_ref, g_ref, t_hbm, x_hbm, top_ref, tot_ref, t_vmem, x_vmem, t_sem, x_sem, flags, *, scale, slots, window):
    arrive, need, finish = load_all(order_ref, t_hbm, x_hbm, t_vmem, x_vmem, t_sem, x_sem, flags, window)

    def step(s, carry):
        arrive(s)
        top_ref[s] = jnp.full(top_ref.shape[1:], VERY_LOW, jnp.float32)
        tot_ref[s] = jnp.zeros(tot_ref.shape[1:], jnp.float32)
        for c in range(slots):

            @pl.when(c < cnt_ref[s])
            def _():
                t = ids_ref[s * slots + c]
                need(t)
                kt = lax.dot_general(t_vmem[t], x_vmem[s], NT_DIMS, preferred_element_type=jnp.float32)
                logits = g_ref[t] + kt * scale
                old = top_ref[s]
                new = jnp.maximum(old, jnp.max(logits, axis=0, keepdims=True))
                tot_ref[s] = tot_ref[s] * jnp.exp(old - new) + jnp.sum(
                    jnp.exp(logits - new), axis=0, keepdims=True
                )
                top_ref[s] = new

        return carry

    lax.fori_loop(0, x_vmem.shape[0], step, 0)
    finish()


def col_kernel(ids_ref, cnt_ref, order_ref, f_ref, t_hbm, x_hbm, top_ref, tot_ref, t_vmem, x_vmem, t_sem, x_sem, flags, *, scale, slots, window):
    arrive, need, finish = load_all(order_ref, t_hbm, x_hbm, t_vmem, x_vmem, t_sem, x_sem, flags, window)
    top_ref[...] = jnp.full(top_ref.shape, VERY_LOW, jnp.float32)
    tot_ref[...] = jnp.zeros(tot_ref.shape, jnp.float32)

    def step(s, carry):
        arrive(s)
        f_row = f_ref[s]
        f_column = jnp.transpose(jnp.broadcast_to(f_row, (128, f_row.shape[1])))[:, :1]
        for c in range(slots):

            @pl.when(c < cnt_ref[s])
            def _():
                t = ids_ref[s * slots + c]
                need(t)
                k = lax.dot_general(x_vmem[s], t_vmem[t], NT_DIMS, preferred_element_type=jnp.float32)
                logits = f_column + k * scale
                old = top_ref[t]
                new = jnp.maximum(old, jnp.max(logits, axis=0, keepdims=True))
                tot_ref[t] = tot_ref[t] * jnp.exp(old - new) + jnp.sum(
                    jnp.exp(logits - new), axis=0, keepdims=True
                )
                top_ref[t] = new

        return carry

    lax.fori_loop(0, x_vmem.shape[0], step, 0)
    finish()


def first_use_order(ids, cnt, tiles):
    blocks, slots = ids.shape
    live = jnp.arange(slots, dtype=jnp.int32)[None, :] < cnt[:, None]
    position = jnp.arange(blocks * slots, dtype=jnp.int32).reshape(blocks, slots)
    hit = (ids[:, :, None] == jnp.arange(tiles, dtype=jnp.int32)) & live[:, :, None]
    first = jnp.min(jnp.where(hit, position[:, :, None], blocks * slots), axis=(0, 1))
    return jnp.argsort(first).astype(jnp.int32)


def resident_call(body, ids, cnt, side, targets, x_all, rows, out_shape, scale):
    tiles, width, depth = targets.shape
    blocks = x_all.shape[0]
    slots = ids.shape[1]
    smem = pl.BlockSpec(memory_space=pltpu.SMEM)
    vmem = pl.BlockSpec(memory_space=pltpu.VMEM)
    hbm = pl.BlockSpec(memory_space=pl.ANY)
    cost = pl.CostEstimate(
        flops=2 * blocks * slots * rows * width * depth,
        transcendentals=blocks * slots * rows * width,
        bytes_accessed=2 * (targets.size + blocks * rows * depth),
    )
    kernel = lambda *refs: body(*refs, scale=scale, slots=slots, window=5)
    return pl.pallas_call(
        kernel,
        out_shape=(out_shape, out_shape),
        in_specs=[smem, smem, smem, vmem, hbm, hbm],
        out_specs=(vmem, vmem),
        scratch_shapes=[
            pltpu.VMEM((tiles, width, depth), targets.dtype),
            pltpu.VMEM((blocks, rows, depth), x_all.dtype),
            pltpu.SemaphoreType.DMA((tiles,)),
            pltpu.SemaphoreType.DMA((blocks,)),
            pltpu.SMEM((tiles,), jnp.int32),
        ],
        compiler_params=pltpu.CompilerParams(vmem_limit_bytes=56 * 1024 * 1024),
        cost_estimate=cost,
    )(ids.reshape(-1), cnt, first_use_order(ids, cnt, tiles), side, targets, x_all)


def local(sources, log_a, targets, g_old, log_b, tile_ids, live_count):
    tiles_own, width, depth = targets.shape
    rows = sources.shape[0]
    slots_per = tile_ids.shape[2]
    groups = tile_ids.shape[1]
    me = lax.axis_index("src")
    scale = 1.0 / (math.sqrt(depth) * EPSILON)

    meta = jnp.concatenate([tile_ids[0].reshape(-1), live_count[0].reshape(-1)])
    x_all = lax.all_gather(sources, "src")
    blocks = x_all.shape[0]
    meta_all = lax.all_to_all(
        jnp.broadcast_to(meta[None], (blocks,) + meta.shape), "src", 0, 0, tiled=True
    )
    ids_all = meta_all[:, : groups * slots_per].reshape(blocks, groups, slots_per)
    cnt_all = meta_all[:, groups * slots_per :]
    my_ids = jnp.clip(lax.dynamic_index_in_dim(ids_all, me, 1, False) - me * tiles_own, 0, tiles_own - 1)
    my_cnt = lax.dynamic_index_in_dim(cnt_all, me, 1, False)

    g_col = (g_old.astype(jnp.float32) / EPSILON)[:, :, None]
    row_top, row_total = resident_call(
        row_kernel, my_ids, my_cnt, g_col, targets, x_all, rows,
        jax.ShapeDtypeStruct((blocks, 1, rows), jnp.float32), scale,
    )
    sent = jnp.stack([row_top.reshape(blocks, rows), row_total.reshape(blocks, rows)], axis=1)
    got = lax.all_to_all(sent, "src", 0, 0, tiled=True)
    top = jnp.max(got[:, 0], axis=0)
    total = jnp.sum(got[:, 1] * jnp.exp(got[:, 0] - top[None]), axis=0)
    f_new = EPSILON * log_a - EPSILON * (top + jnp.log(total))
    f_all = lax.all_to_all(
        jnp.broadcast_to(f_new[None], (blocks,) + f_new.shape), "src", 0, 0, tiled=True
    )

    f_col = (f_all / EPSILON)[:, None, :]
    tile_top, tile_total = resident_call(
        col_kernel, my_ids, my_cnt, f_col, targets, x_all, rows,
        jax.ShapeDtypeStruct((tiles_own, 1, width), jnp.float32), scale,
    )
    col = jnp.concatenate([tile_top.reshape(tiles_own, width), tile_total.reshape(tiles_own, width)])
    loop_size = lax.axis_size("loop")
    col_all = lax.all_to_all(
        jnp.broadcast_to(col[None], (loop_size,) + col.shape), "loop", 0, 0, tiled=True
    )
    tops = col_all[:, :tiles_own]
    all_top = jnp.max(tops, axis=0)
    all_total = jnp.sum(col_all[:, tiles_own:] * jnp.exp(tops - all_top[None]), axis=0)
    g_new = EPSILON * log_b - EPSILON * (all_top + jnp.log(all_total))
    return (f_new, g_new)


def solution(mesh):
    return jax.shard_map(
        local,
        mesh=mesh,
        in_specs=(
            P(("src", "loop"), None),
            P(("src", "loop")),
            P("src", None, None),
            P("src", None),
            P("src", None),
            P(("src", "loop"), None, None),
            P(("src", "loop"), None),
        ),
        out_specs=(P(("src", "loop")), P("src", None)),
        check_vma=False,
    )
```

```python
import math

import jax
import jax.numpy as jnp
from jax import lax
from jax.experimental import pallas as pl
from jax.experimental.pallas import tpu as pltpu
from jax.sharding import PartitionSpec as P

EPSILON = 0.1
VERY_LOW = -1e30
NT_DIMS = (((1,), (1,)), ((), ()))


def load_all(order_ref, t_hbm, x_hbm, t_vmem, x_vmem, t_sem, x_sem, flags, window):
    tiles, blocks = t_vmem.shape[0], x_vmem.shape[0]
    rows = x_vmem.shape[1]

    def x_copy(s):
        return pltpu.make_async_copy(x_hbm.at[s, pl.ds(0, rows)], x_vmem.at[s], x_sem.at[s])

    def t_copy(t):
        return pltpu.make_async_copy(t_hbm.at[t], t_vmem.at[t], t_sem.at[t])

    for t in range(tiles):
        flags[t] = 0
    issue = [("x", 0), ("t", 0), ("t", 1), ("x", 1), ("t", 2), ("x", 2), ("t", 3), ("x", 3)]
    issue = [item for item in issue if item[1] < (min(window, blocks) if item[0] == "x" else tiles)]
    issue += [("x", s) for s in range(4, min(window, blocks))]
    issue += [("t", k) for k in range(4, tiles)]
    for kind, k in issue:
        if kind == "x":
            x_copy(k).start()
        else:
            t_copy(order_ref[k]).start()

    def arrive(s):
        x_copy(s).wait()

        @pl.when(s + window < blocks)
        def _():
            x_copy(jnp.minimum(s + window, blocks - 1)).start()

    def need(t):
        @pl.when(flags[t] == 0)
        def _():
            t_copy(t).wait()
            flags[t] = 1

    def finish():
        for t in range(tiles):
            need(t)

    return arrive, need, finish


def row_kernel(ids_ref, cnt_ref, order_ref, g_ref, t_hbm, x_hbm, top_ref, tot_ref, t_vmem, x_vmem, t_sem, x_sem, flags, *, scale, slots, window):
    arrive, need, finish = load_all(order_ref, t_hbm, x_hbm, t_vmem, x_vmem, t_sem, x_sem, flags, window)

    def step(s, carry):
        arrive(s)
        top_ref[s] = jnp.full(top_ref.shape[1:], VERY_LOW, jnp.float32)
        tot_ref[s] = jnp.zeros(tot_ref.shape[1:], jnp.float32)
        for c in range(slots):

            @pl.when(c < cnt_ref[s])
            def _():
                t = ids_ref[s * slots + c]
                need(t)
                kt = lax.dot_general(t_vmem[t], x_vmem[s], NT_DIMS, preferred_element_type=jnp.float32)
                logits = g_ref[t] + kt * scale
                old = top_ref[s]
                new = jnp.maximum(old, jnp.max(logits, axis=0, keepdims=True))
                tot_ref[s] = tot_ref[s] * jnp.exp(old - new) + jnp.sum(
                    jnp.exp(logits - new), axis=0, keepdims=True
                )
                top_ref[s] = new

        return carry

    lax.fori_loop(0, x_vmem.shape[0], step, 0)
    finish()


def col_kernel(ids_ref, cnt_ref, order_ref, f_ref, t_hbm, x_hbm, top_ref, tot_ref, t_vmem, x_vmem, t_sem, x_sem, flags, *, scale, slots, window):
    arrive, need, finish = load_all(order_ref, t_hbm, x_hbm, t_vmem, x_vmem, t_sem, x_sem, flags, window)
    top_ref[...] = jnp.full(top_ref.shape, VERY_LOW, jnp.float32)
    tot_ref[...] = jnp.zeros(tot_ref.shape, jnp.float32)

    def step(s, carry):
        arrive(s)
        f_row = f_ref[s]
        f_column = jnp.transpose(jnp.broadcast_to(f_row, (128, f_row.shape[1])))[:, :1]
        for c in range(slots):

            @pl.when(c < cnt_ref[s])
            def _():
                t = ids_ref[s * slots + c]
                need(t)
                k = lax.dot_general(x_vmem[s], t_vmem[t], NT_DIMS, preferred_element_type=jnp.float32)
                logits = f_column + k * scale
                old = top_ref[t]
                new = jnp.maximum(old, jnp.max(logits, axis=0, keepdims=True))
                tot_ref[t] = tot_ref[t] * jnp.exp(old - new) + jnp.sum(
                    jnp.exp(logits - new), axis=0, keepdims=True
                )
                top_ref[t] = new

        return carry

    lax.fori_loop(0, x_vmem.shape[0], step, 0)
    finish()


def first_use_order(ids, cnt, tiles):
    blocks, slots = ids.shape
    live = jnp.arange(slots, dtype=jnp.int32)[None, :] < cnt[:, None]
    position = jnp.arange(blocks * slots, dtype=jnp.int32).reshape(blocks, slots)
    hit = (ids[:, :, None] == jnp.arange(tiles, dtype=jnp.int32)) & live[:, :, None]
    first = jnp.min(jnp.where(hit, position[:, :, None], blocks * slots), axis=(0, 1))
    return jnp.argsort(first).astype(jnp.int32)


def resident_call(body, ids, cnt, side, targets, x_all, rows, out_shape, scale):
    tiles, width, depth = targets.shape
    blocks = x_all.shape[0]
    slots = ids.shape[1]
    smem = pl.BlockSpec(memory_space=pltpu.SMEM)
    vmem = pl.BlockSpec(memory_space=pltpu.VMEM)
    hbm = pl.BlockSpec(memory_space=pl.ANY)
    cost = pl.CostEstimate(
        flops=2 * blocks * slots * rows * width * depth,
        transcendentals=blocks * slots * rows * width,
        bytes_accessed=2 * (targets.size + blocks * rows * depth),
    )
    kernel = lambda *refs: body(*refs, scale=scale, slots=slots, window=7)
    return pl.pallas_call(
        kernel,
        out_shape=(out_shape, out_shape),
        in_specs=[smem, smem, smem, vmem, hbm, hbm],
        out_specs=(vmem, vmem),
        scratch_shapes=[
            pltpu.VMEM((tiles, width, depth), targets.dtype),
            pltpu.VMEM((blocks, rows, depth), x_all.dtype),
            pltpu.SemaphoreType.DMA((tiles,)),
            pltpu.SemaphoreType.DMA((blocks,)),
            pltpu.SMEM((tiles,), jnp.int32),
        ],
        compiler_params=pltpu.CompilerParams(vmem_limit_bytes=56 * 1024 * 1024),
        cost_estimate=cost,
    )(ids.reshape(-1), cnt, first_use_order(ids, cnt, tiles), side, targets, x_all)


def local(sources, log_a, targets, g_old, log_b, tile_ids, live_count):
    tiles_own, width, depth = targets.shape
    rows = sources.shape[0]
    slots_per = tile_ids.shape[2]
    groups = tile_ids.shape[1]
    me = lax.axis_index("src")
    scale = 1.0 / (math.sqrt(depth) * EPSILON)

    meta = jnp.concatenate([tile_ids[0].reshape(-1), live_count[0].reshape(-1)])
    x_all = lax.all_gather(sources, "src")
    blocks = x_all.shape[0]
    meta_all = lax.all_to_all(
        jnp.broadcast_to(meta[None], (blocks,) + meta.shape), "src", 0, 0, tiled=True
    )
    ids_all = meta_all[:, : groups * slots_per].reshape(blocks, groups, slots_per)
    cnt_all = meta_all[:, groups * slots_per :]
    my_ids = jnp.clip(lax.dynamic_index_in_dim(ids_all, me, 1, False) - me * tiles_own, 0, tiles_own - 1)
    my_cnt = lax.dynamic_index_in_dim(cnt_all, me, 1, False)

    g_col = (g_old.astype(jnp.float32) / EPSILON)[:, :, None]
    row_top, row_total = resident_call(
        row_kernel, my_ids, my_cnt, g_col, targets, x_all, rows,
        jax.ShapeDtypeStruct((blocks, 1, rows), jnp.float32), scale,
    )
    sent = jnp.stack([row_top.reshape(blocks, rows), row_total.reshape(blocks, rows)], axis=1)
    got = lax.all_to_all(sent, "src", 0, 0, tiled=True)
    top = jnp.max(got[:, 0], axis=0)
    total = jnp.sum(got[:, 1] * jnp.exp(got[:, 0] - top[None]), axis=0)
    f_new = EPSILON * log_a - EPSILON * (top + jnp.log(total))
    f_all = lax.all_to_all(
        jnp.broadcast_to(f_new[None], (blocks,) + f_new.shape), "src", 0, 0, tiled=True
    )

    f_col = (f_all / EPSILON)[:, None, :]
    tile_top, tile_total = resident_call(
        col_kernel, my_ids, my_cnt, f_col, targets, x_all, rows,
        jax.ShapeDtypeStruct((tiles_own, 1, width), jnp.float32), scale,
    )
    col = jnp.concatenate([tile_top.reshape(tiles_own, width), tile_total.reshape(tiles_own, width)])
    loop_size = lax.axis_size("loop")
    col_all = lax.all_to_all(
        jnp.broadcast_to(col[None], (loop_size,) + col.shape), "loop", 0, 0, tiled=True
    )
    tops = col_all[:, :tiles_own]
    all_top = jnp.max(tops, axis=0)
    all_total = jnp.sum(col_all[:, tiles_own:] * jnp.exp(tops - all_top[None]), axis=0)
    g_new = EPSILON * log_b - EPSILON * (all_top + jnp.log(all_total))
    return (f_new, g_new)


def solution(mesh):
    return jax.shard_map(
        local,
        mesh=mesh,
        in_specs=(
            P(("src", "loop"), None),
            P(("src", "loop")),
            P("src", None, None),
            P("src", None),
            P("src", None),
            P(("src", "loop"), None, None),
            P(("src", "loop"), None),
        ),
        out_specs=(P(("src", "loop")), P("src", None)),
        check_vma=False,
    )
```
